128 devices in a mesh: layer: 16 (over y, x), prow: 4 (over z), pcol: 2 (over core).
Axes of the slice: x: 4, y: 4, z: 4, core: 2. Of those that a mesh axis runs over, the one named last changes fastest.
Arguments:
- front: bfloat16 [16, 2048, 32768], P('layer', 'prow', 'pcol'), may hold values from -6 to 6
- pivots: bfloat16 [16, 2, 256, 32768], P('layer', None, 'prow', 'pcol'), may hold values from -0.8984375 to 0.8984375
- inverses: bfloat16 [16, 2, 256, 256], P('layer'), may hold values from -0.1875 to 0.1875
- slab_pattern: int32 [16, 8, 128], P('layer', 'prow', 'pcol'), may hold values 0 or 1
- pivot_pattern: int32 [16, 2, 128], P('layer', None, 'pcol'), may hold values from 0 to 1, as said below
Outputs:
- ancestor: float32 [4, 16, 32, 32768], P('prow', 'layer', None, 'pcol')
- lower: bfloat16 [16, 2048, 512], P('layer', 'prow')
- upper: bfloat16 [16, 256, 32768], P('layer', 'prow', 'pcol')
The draws below stay inside these ranges and needn't reach their ends.
Inputs may be any that keep to these rules, and one draw needn't show every extreme that they name: `pivot_pattern`: each entry says whether that block of the pivot rows is structurally nonzero. `slab_pattern`: each entry says whether that block of the front rows is structurally nonzero.
All inputs are finite; a program needn't handle non-finite values.
Results may differ from the reference program's by a relative error of at most 0.014.
Values may be sent and summed in bfloat16 or wider, within the bound.
No kernel may reach another device: no remote copies, remote signals or barrier semaphores. Data moves between devices by JAX's collectives and lax.ppermute only.
A program may use at most 192 MiB of HBM per device.

```python
import jax
import jax.numpy as jnp

M = 32768
BLK = 256
PANELS = 2
ROWS_DEV = 512
LAYERS = 16
ROWS = 2048
N_LAYER = 16
N_PROW = 4


def draw_pivot_pattern(key, part):
    col_blocks = M // BLK
    density = 2 + 6 * jnp.arange(col_blocks, dtype=jnp.int32) // col_blocks
    raw_draws = jax.random.randint(key, (LAYERS, PANELS, col_blocks), 0, 8)
    return (raw_draws < density[None, None, :]).astype(jnp.int32)


def plant(array, key, smallest, high):
    longest = array.shape.index(max(array.shape))
    spots = []
    for shift in (0, 1):
        where = [jax.random.randint(jax.random.fold_in(key, axis), (), 0, length) for axis, length in enumerate(array.shape)]
        where[longest] = (where[longest] + shift) % array.shape[longest]
        spots.append(tuple(where))
    return array.at[spots[0]].set(smallest).at[spots[1]].set(high)


def level_of(key, dims, cuts, low, largest):
    factor_of, own = 1.0, jax.random.fold_in(key, 6)
    for position, shards_of in cuts:
        draws = jnp.exp(jax.random.uniform(jax.random.fold_in(own, position), (shards_of,), jnp.float32, low / len(cuts), largest / len(cuts)))
        factor_of = factor_of * jnp.repeat(draws, dims[position] // shards_of).reshape([-1 if axis == position else 1 for axis in range(len(dims))])
    return factor_of


def bell_draw(key, extent, spread, limit, cuts=(), held_as=jnp.bfloat16):
    values = spread * jax.random.normal(key, extent, jnp.float32)
    if cuts:
        values = values * level_of(key, extent, cuts, -0.22, 0.18)
    return jnp.clip(values, -limit, limit).astype(held_as)


def setup_inputs(seed: int = 0) -> dict:
    seeds = jax.random.split(jax.random.key(seed), 6)
    front = bell_draw(seeds[0], (LAYERS, ROWS, M), 1.0, 6.0, ((0, 16), (1, 4), (2, 2)))
    pivots = bell_draw(seeds[1], (LAYERS, PANELS, BLK, M), 0.15, 0.8984375, ((0, 16), (2, 4), (3, 2)))
    inverses = bell_draw(seeds[2], (LAYERS, PANELS, BLK, BLK), (4 * BLK) ** -0.5, 0.1875, ((0, 16),))
    slab_pattern = plant((jax.random.randint(seeds[3], (LAYERS, ROWS // BLK, M // BLK), 0, 4) < 3).astype(jnp.int32), jax.random.fold_in(seeds[3], 1), 0, 1)
    pivot_pattern = draw_pivot_pattern(jax.random.fold_in(seeds[5], 71), 0)
    return {"front": front, "pivots": pivots, "inverses": inverses, "slab_pattern": slab_pattern, "pivot_pattern": pivot_pattern}


def one_layer(front, pivots, inverses, slab_pattern, pivot_pattern):
    row_total = front.shape[0]
    col_blocks = M // BLK
    panel_width = PANELS * BLK
    masked = (front.reshape(row_total // BLK, BLK, col_blocks, BLK) * slab_pattern.astype(jnp.bfloat16)[:, None, :, None]).reshape(row_total, M)
    pivot_masked = (pivots.reshape(PANELS, BLK, col_blocks, BLK) * pivot_pattern.astype(jnp.bfloat16)[:, None, None, :, None][:, 0]).reshape(PANELS, BLK, M)
    upper_first = pivot_masked[0]
    second_rows = pivot_masked[1]
    lower_pivot = jnp.dot(second_rows[:, :BLK], inverses[0], preferred_element_type=jnp.float32).astype(jnp.bfloat16)
    upper_second = (second_rows.astype(jnp.float32) - jnp.dot(lower_pivot, upper_first, preferred_element_type=jnp.float32)).astype(jnp.bfloat16)
    lower_first = jnp.dot(masked[:, :BLK], inverses[0], preferred_element_type=jnp.float32).astype(jnp.bfloat16)
    carried = (masked[:, BLK:panel_width].astype(jnp.float32) - jnp.dot(lower_first, upper_first[:, BLK:panel_width], preferred_element_type=jnp.float32)).astype(jnp.bfloat16)
    lower_second = jnp.dot(carried, inverses[1], preferred_element_type=jnp.float32).astype(jnp.bfloat16)
    lower_panel = jnp.concatenate([lower_first, lower_second], 1)
    stacked = jnp.concatenate([upper_first, upper_second], 0)
    schur_rows = masked.astype(jnp.float32) - jnp.dot(lower_panel, stacked, preferred_element_type=jnp.float32)
    retained = jnp.arange(M) >= panel_width
    schur_rows = jnp.where(retained[None, :], schur_rows, jnp.zeros_like(schur_rows))
    return schur_rows, lower_panel, upper_second


def reference(front, pivots, inverses, slab_pattern, pivot_pattern):
    summed = jnp.zeros((N_PROW * ROWS_DEV, M), jnp.float32)
    lower_list = []
    upper_list = []
    for layer_index in range(LAYERS):
        schur_rows, lower_panel, upper_second = one_layer(front[layer_index], pivots[layer_index], inverses[layer_index], slab_pattern[layer_index], pivot_pattern[layer_index])
        summed = summed + schur_rows
        lower_list.append(lower_panel)
        upper_list.append(upper_second)
    ancestor = summed.reshape(N_PROW, N_LAYER, ROWS_DEV // N_LAYER, M)
    return ancestor, jnp.stack(lower_list), jnp.stack(upper_list)
```

```python
import jax
import jax.numpy as jnp
from jax import lax
from jax.sharding import PartitionSpec as P

CHUNKS = 4


def ring(value, axis, size, step):
    return lax.ppermute(value, axis, [(i, (i + step) % size) for i in range(size)])


def gather_relative(value, axis, size):
    from_prev = ring(value, axis, size, 1)
    from_next = ring(value, axis, size, -1)
    half = value.shape[1] // 2
    far_lo = ring(from_prev[:, :half], axis, size, 1)
    far_hi = ring(from_next[:, half:], axis, size, -1)
    far = jnp.concatenate([far_lo, far_hi], 1)
    return jnp.concatenate([value, from_next, far, from_prev], 1)


def on_device(front, pivots, inverses, slab_pattern, pivot_pattern):
    block_size = inverses.shape[-1]
    panel_width = 2 * block_size
    row_count = front.shape[1]
    col_count = front.shape[2]
    own_rows = pivots.shape[2]
    n_prow = lax.axis_size("prow")
    n_pcol = lax.axis_size("pcol")
    assert n_prow == 4
    masked = (
        front[0].reshape(row_count // block_size, block_size, col_count // block_size, block_size)
        * slab_pattern[0].astype(jnp.bfloat16)[:, None, :, None]
    ).reshape(row_count, col_count)
    pivot_masked = (
        pivots[0].reshape(2, own_rows, col_count // block_size, block_size)
        * pivot_pattern[0].astype(jnp.bfloat16)[:, None, :, None]
    ).reshape(2, own_rows, col_count)
    first_inverse = inverses[0, 0]
    second_inverse = inverses[0, 1]
    prow = lax.axis_index("prow")
    pcol = lax.axis_index("pcol")

    panel = lax.all_gather(pivot_masked[:, :, :panel_width], "prow", axis=1, tiled=True)
    lower_pivot = jnp.dot(
        panel[1][:, :block_size], first_inverse, preferred_element_type=jnp.float32
    ).astype(jnp.bfloat16)
    lower_first = jnp.dot(
        masked[:, :block_size], first_inverse, preferred_element_type=jnp.float32
    ).astype(jnp.bfloat16)
    carried = (
        masked[:, block_size:panel_width].astype(jnp.float32)
        - jnp.dot(
            lower_first, panel[0][:, block_size:panel_width], preferred_element_type=jnp.float32
        )
    ).astype(jnp.bfloat16)
    lower_second = jnp.dot(carried, second_inverse, preferred_element_type=jnp.float32).astype(
        jnp.bfloat16
    )
    lower_panel = jnp.concatenate([lower_first, lower_second], 1)
    sent = lax.ppermute((lower_panel, lower_pivot), "pcol", [(0, i) for i in range(1, n_pcol)])
    on_root = pcol == 0
    lower_panel = jnp.where(on_root, lower_panel, sent[0])
    lower_pivot = jnp.where(on_root, lower_pivot, sent[1])

    shift = prow * own_rows
    lower_rel = jnp.concatenate(
        [
            jnp.roll(lower_panel[:, :block_size], -shift, axis=1),
            jnp.roll(lower_panel[:, block_size:], -shift, axis=1),
        ],
        1,
    )
    pivot_rel = jnp.roll(jnp.roll(lower_pivot, -shift, axis=0), -shift, axis=1)

    width = col_count // CHUNKS
    summed_parts = []
    upper_parts = []
    for k in range(CHUNKS):
        cols = slice(k * width, (k + 1) * width)
        rows_rel = gather_relative(pivot_masked[:, :, cols], "prow", n_prow)
        first_rel = rows_rel[0]
        upper_rel = (
            rows_rel[1].astype(jnp.float32)
            - jnp.dot(pivot_rel, first_rel, preferred_element_type=jnp.float32)
        ).astype(jnp.bfloat16)
        upper_parts.append(upper_rel[:own_rows])
        stacked = jnp.concatenate([first_rel, upper_rel], 0)
        col_index = pcol * col_count + k * width + jnp.arange(width, dtype=jnp.int32)
        retained = col_index >= panel_width
        schur = masked[:, cols].astype(jnp.float32) - jnp.dot(
            lower_rel, stacked, preferred_element_type=jnp.float32
        )
        schur = jnp.where(retained[None, :], schur, jnp.zeros_like(schur))
        summed_parts.append(
            lax.psum_scatter(schur.astype(jnp.bfloat16), "layer", scatter_dimension=0, tiled=True)
        )
    summed = jnp.concatenate(summed_parts, 1).astype(jnp.float32)
    ancestor = summed.reshape(1, 1, summed.shape[0], col_count)
    upper_own = jnp.concatenate(upper_parts, 1)
    return (ancestor, lower_panel[None], upper_own[None])


def solution(mesh):
    placed = (
        P("layer", "prow", "pcol"),
        P("layer", None, "prow", "pcol"),
        P("layer", None, None, None),
        P("layer", "prow", "pcol"),
        P("layer", None, "pcol"),
    )
    return jax.shard_map(
        on_device,
        mesh=mesh,
        in_specs=placed,
        out_specs=(
            P("prow", "layer", None, "pcol"),
            P("layer", "prow", None),
            P("layer", "prow", "pcol"),
        ),
        check_vma=False,
    )
```

```python
import jax
import jax.numpy as jnp
from jax import lax
from jax.sharding import PartitionSpec as P

CHUNKS = 4


def ring(value, axis, size, step):
    return lax.ppermute(value, axis, [(i, (i + step) % size) for i in range(size)])


def gather_relative(value, axis, size):
    from_prev = ring(value, axis, size, 1)
    from_next = ring(value, axis, size, -1)
    half = value.shape[1] // 2
    far_lo = ring(from_prev[:, :half], axis, size, 1)
    far_hi = ring(from_next[:, half:], axis, size, -1)
    far = jnp.concatenate([far_lo, far_hi], 1)
    return jnp.concatenate([value, from_next, far, from_prev], 1)


def grid_shift(value, axis, side, dy, dx):
    pairs = []
    for y in range(side):
        for x in range(side):
            pairs.append((y * side + x, ((y + dy) % side) * side + (x + dx) % side))
    return lax.ppermute(value, axis, pairs)


def ring_reduce(blocks, send):
    half = blocks.shape[1] // 2
    far = blocks[2].astype(jnp.bfloat16)
    fwd1 = send(far[:half], 1)
    bwd1 = send(far[half:], -1)
    next_block = blocks[1]
    prev_block = blocks[3]
    fwd2 = send(
        jnp.concatenate([next_block[:half] + fwd1.astype(jnp.float32), next_block[half:]], 0).astype(
            jnp.bfloat16
        ),
        1,
    )
    bwd2 = send(
        jnp.concatenate([prev_block[:half], prev_block[half:] + bwd1.astype(jnp.float32)], 0).astype(
            jnp.bfloat16
        ),
        -1,
    )
    return blocks[0] + fwd2.astype(jnp.float32) + bwd2.astype(jnp.float32)


def relative(value, own, axis):
    return jnp.stack(
        [lax.dynamic_index_in_dim(value, (own + j) % 4, axis, keepdims=False) for j in range(4)], 0
    )


def grid_reduce_scatter(schur, axis):
    side = 4
    index = lax.axis_index(axis)
    gy = index // side
    gx = index % side
    rows, width = schur.shape
    part = rows // (side * side)
    grid = schur.reshape(side, side, part, width)
    left = grid[..., : width // 2]
    right = grid[..., width // 2 :]

    def along_x(v, step):
        return grid_shift(v, axis, side, 0, step)

    def along_y(v, step):
        return grid_shift(v, axis, side, step, 0)

    left = ring_reduce(relative(left, gx, 1), along_x)
    left = ring_reduce(relative(left, gy, 0), along_y)
    right = ring_reduce(relative(right, gy, 0), along_y)
    right = ring_reduce(relative(right, gx, 0), along_x)
    return jnp.concatenate([left, right], 1)


def on_device(front, pivots, inverses, slab_pattern, pivot_pattern):
    block_size = inverses.shape[-1]
    panel_width = 2 * block_size
    row_count = front.shape[1]
    col_count = front.shape[2]
    own_rows = pivots.shape[2]
    n_prow = lax.axis_size("prow")
    n_pcol = lax.axis_size("pcol")
    assert n_prow == 4
    masked = (
        front[0].reshape(row_count // block_size, block_size, col_count // block_size, block_size)
        * slab_pattern[0].astype(jnp.bfloat16)[:, None, :, None]
    ).reshape(row_count, col_count)
    pivot_masked = (
        pivots[0].reshape(2, own_rows, col_count // block_size, block_size)
        * pivot_pattern[0].astype(jnp.bfloat16)[:, None, :, None]
    ).reshape(2, own_rows, col_count)
    first_inverse = inverses[0, 0]
    second_inverse = inverses[0, 1]
    prow = lax.axis_index("prow")
    pcol = lax.axis_index("pcol")

    panel = jnp.roll(
        gather_relative(pivot_masked[:, :, :panel_width], "prow", n_prow), prow * own_rows, axis=1
    )
    lower_pivot = jnp.dot(
        panel[1][:, :block_size], first_inverse, preferred_element_type=jnp.float32
    ).astype(jnp.bfloat16)
    lower_first = jnp.dot(
        masked[:, :block_size], first_inverse, preferred_element_type=jnp.float32
    ).astype(jnp.bfloat16)
    carried = (
        masked[:, block_size:panel_width].astype(jnp.float32)
        - jnp.dot(
            lower_first, panel[0][:, block_size:panel_width], preferred_element_type=jnp.float32
        )
    ).astype(jnp.bfloat16)
    lower_second = jnp.dot(carried, second_inverse, preferred_element_type=jnp.float32).astype(
        jnp.bfloat16
    )
    lower_panel = jnp.concatenate([lower_first, lower_second], 1)
    sent = lax.ppermute((lower_panel, lower_pivot), "pcol", [(0, i) for i in range(1, n_pcol)])
    on_root = pcol == 0
    lower_panel = jnp.where(on_root, lower_panel, sent[0])
    lower_pivot = jnp.where(on_root, lower_pivot, sent[1])

    shift = prow * own_rows
    lower_rel = jnp.concatenate(
        [
            jnp.roll(lower_panel[:, :block_size], -shift, axis=1),
            jnp.roll(lower_panel[:, block_size:], -shift, axis=1),
        ],
        1,
    )
    pivot_rel = jnp.roll(jnp.roll(lower_pivot, -shift, axis=0), -shift, axis=1)

    width = col_count // CHUNKS
    summed_parts = []
    upper_parts = []
    for k in range(CHUNKS):
        cols = slice(k * width, (k + 1) * width)
        rows_rel = gather_relative(pivot_masked[:, :, cols], "prow", n_prow)
        first_rel = rows_rel[0]
        upper_rel = (
            rows_rel[1].astype(jnp.float32)
            - jnp.dot(pivot_rel, first_rel, preferred_element_type=jnp.float32)
        ).astype(jnp.bfloat16)
        upper_parts.append(upper_rel[:own_rows])
        stacked = jnp.concatenate([first_rel, upper_rel], 0)
        col_index = pcol * col_count + k * width + jnp.arange(width, dtype=jnp.int32)
        retained = col_index >= panel_width
        schur = masked[:, cols].astype(jnp.float32) - jnp.dot(
            lower_rel, stacked, preferred_element_type=jnp.float32
        )
        schur = jnp.where(retained[None, :], schur, jnp.zeros_like(schur))
        summed_parts.append(grid_reduce_scatter(schur, "layer"))
    summed = jnp.concatenate(summed_parts, 1)
    ancestor = summed.reshape(1, 1, summed.shape[0], col_count)
    upper_own = jnp.concatenate(upper_parts, 1)
    return (ancestor, lower_panel[None], upper_own[None])


def solution(mesh):
    placed = (
        P("layer", "prow", "pcol"),
        P("layer", None, "prow", "pcol"),
        P("layer", None, None, None),
        P("layer", "prow", "pcol"),
        P("layer", None, "pcol"),
    )
    return jax.shard_map(
        on_device,
        mesh=mesh,
        in_specs=placed,
        out_specs=(
            P("prow", "layer", None, "pcol"),
            P("layer", "prow", None),
            P("layer", "prow", "pcol"),
        ),
        check_vma=False,
    )
```

```python
import jax
import jax.numpy as jnp
from jax import lax
from jax.sharding import PartitionSpec as P


def ring(value, axis, size, step):
    return lax.ppermute(value, axis, [(i, (i + step) % size) for i in range(size)])


def gather_relative(value, axis, size):
    from_prev = ring(value, axis, size, 1)
    from_next = ring(value, axis, size, -1)
    half = value.shape[1] // 2
    far_lo = ring(from_prev[:, :half], axis, size, 1)
    far_hi = ring(from_next[:, half:], axis, size, -1)
    far = jnp.concatenate([far_lo, far_hi], 1)
    return jnp.concatenate([value, from_next, far, from_prev], 1)


def on_device(front, pivots, inverses, slab_pattern, pivot_pattern):
    block_size = inverses.shape[-1]
    panel_width = 2 * block_size
    row_count = front.shape[1]
    col_count = front.shape[2]
    own_rows = pivots.shape[2]
    masked = (
        front[0].reshape(row_count // block_size, block_size, col_count // block_size, block_size)
        * slab_pattern[0].astype(jnp.bfloat16)[:, None, :, None]
    ).reshape(row_count, col_count)
    pivot_masked = (
        pivots[0].reshape(2, own_rows, col_count // block_size, block_size)
        * pivot_pattern[0].astype(jnp.bfloat16)[:, None, :, None]
    ).reshape(2, own_rows, col_count)
    first_inverse = inverses[0, 0]
    second_inverse = inverses[0, 1]
    row_offset = lax.axis_index("prow") * own_rows
    pcol = lax.axis_index("pcol")
    n_prow = lax.axis_size("prow")
    n_pcol = lax.axis_size("pcol")
    assert n_prow == 4
    gathered = lax.all_gather(pivot_masked, "prow", axis=1, tiled=True)
    panel = jnp.roll(
        gather_relative(pivot_masked[:, :, :panel_width], "prow", n_prow), row_offset, axis=1
    )
    front_cols = masked[:, :panel_width]
    pivot_cols = panel[0]
    second_cols = panel[1]
    lower_pivot = jnp.dot(
        second_cols[:, :block_size], first_inverse, preferred_element_type=jnp.float32
    ).astype(jnp.bfloat16)
    lower_first = jnp.dot(
        front_cols[:, :block_size], first_inverse, preferred_element_type=jnp.float32
    ).astype(jnp.bfloat16)
    carried = (
        front_cols[:, block_size:].astype(jnp.float32)
        - jnp.dot(
            lower_first, pivot_cols[:, block_size:panel_width], preferred_element_type=jnp.float32
        )
    ).astype(jnp.bfloat16)
    lower_second = jnp.dot(carried, second_inverse, preferred_element_type=jnp.float32).astype(
        jnp.bfloat16
    )
    lower_panel = jnp.concatenate([lower_first, lower_second], 1)
    sent = lax.ppermute((lower_panel, lower_pivot), "pcol", [(0, i) for i in range(1, n_pcol)])
    on_root = pcol == 0
    lower_panel = jnp.where(on_root, lower_panel, sent[0])
    lower_pivot = jnp.where(on_root, lower_pivot, sent[1])
    upper_first = gathered[0]
    upper_second = (
        gathered[1].astype(jnp.float32)
        - jnp.dot(lower_pivot, upper_first, preferred_element_type=jnp.float32)
    ).astype(jnp.bfloat16)
    upper_own = lax.dynamic_slice_in_dim(upper_second, row_offset, own_rows, 0)
    stacked = jnp.concatenate([upper_first, upper_second], 0)
    col_index = lax.axis_index("pcol") * col_count + jnp.arange(col_count, dtype=jnp.int32)
    retained = col_index >= panel_width
    schur_rows = masked.astype(jnp.float32) - jnp.dot(
        lower_panel, stacked, preferred_element_type=jnp.float32
    )
    schur_rows = jnp.where(retained[None, :], schur_rows, jnp.zeros_like(schur_rows))
    summed = lax.psum_scatter(
        schur_rows.astype(jnp.bfloat16), "layer", scatter_dimension=0, tiled=True
    ).astype(jnp.float32)
    ancestor = summed.reshape(1, 1, summed.shape[0], col_count)
    return (ancestor, lower_panel[None], upper_own[None])


def solution(mesh):
    placed = (
        P("layer", "prow", "pcol"),
        P("layer", None, "prow", "pcol"),
        P("layer", None, None, None),
        P("layer", "prow", "pcol"),
        P("layer", None, "pcol"),
    )
    return jax.shard_map(
        on_device,
        mesh=mesh,
        in_specs=placed,
        out_specs=(
            P("prow", "layer", None, "pcol"),
            P("layer", "prow", None),
            P("layer", "prow", "pcol"),
        ),
        check_vma=False,
    )
```

```python
import jax
import jax.numpy as jnp
from jax import lax
from jax.sharding import PartitionSpec as P


def ring(value, axis, size, step):
    return lax.ppermute(value, axis, [(i, (i + step) % size) for i in range(size)])


def gather_relative(value, axis, size):
    from_prev = ring(value, axis, size, 1)
    from_next = ring(value, axis, size, -1)
    half = value.shape[1] // 2
    far_lo = ring(from_prev[:, :half], axis, size, 1)
    far_hi = ring(from_next[:, half:], axis, size, -1)
    far = jnp.concatenate([far_lo, far_hi], 1)
    return jnp.concatenate([value, from_next, far, from_prev], 1)


def on_device(front, pivots, inverses, slab_pattern, pivot_pattern):
    block_size = inverses.shape[-1]
    panel_width = 2 * block_size
    row_count = front.shape[1]
    col_count = front.shape[2]
    own_rows = pivots.shape[2]
    masked = (
        front[0].reshape(row_count // block_size, block_size, col_count // block_size, block_size)
        * slab_pattern[0].astype(jnp.bfloat16)[:, None, :, None]
    ).reshape(row_count, col_count)
    pivot_masked = (
        pivots[0].reshape(2, own_rows, col_count // block_size, block_size)
        * pivot_pattern[0].astype(jnp.bfloat16)[:, None, :, None]
    ).reshape(2, own_rows, col_count)
    first_inverse = inverses[0, 0]
    second_inverse = inverses[0, 1]
    row_offset = lax.axis_index("prow") * own_rows
    pcol = lax.axis_index("pcol")
    n_prow = lax.axis_size("prow")
    n_pcol = lax.axis_size("pcol")
    assert n_prow == 4
    gathered = lax.all_gather(pivot_masked, "prow", axis=1, tiled=True)
    panel = jnp.roll(
        gather_relative(pivot_masked[:, :, :panel_width], "prow", n_prow), row_offset, axis=1
    )
    front_cols = masked[:, :panel_width]
    pivot_cols = panel[0]
    second_cols = panel[1]
    lower_pivot = jnp.dot(
        second_cols[:, :block_size], first_inverse, preferred_element_type=jnp.float32
    ).astype(jnp.bfloat16)
    lower_first = jnp.dot(
        front_cols[:, :block_size], first_inverse, preferred_element_type=jnp.float32
    ).astype(jnp.bfloat16)
    carried = (
        front_cols[:, block_size:].astype(jnp.float32)
        - jnp.dot(
            lower_first, pivot_cols[:, block_size:panel_width], preferred_element_type=jnp.float32
        )
    ).astype(jnp.bfloat16)
    lower_second = jnp.dot(carried, second_inverse, preferred_element_type=jnp.float32).astype(
        jnp.bfloat16
    )
    lower_panel = jnp.concatenate([lower_first, lower_second], 1)
    sent = lax.ppermute((lower_panel, lower_pivot), "pcol", [(0, i) for i in range(1, n_pcol)])
    on_root = pcol == 0
    lower_panel = jnp.where(on_root, lower_panel, sent[0])
    lower_pivot = jnp.where(on_root, lower_pivot, sent[1])
    own_pivot = lax.dynamic_slice_in_dim(lower_pivot, row_offset, own_rows, 0)
    upper_own = (
        pivot_masked[1].astype(jnp.float32)
        - jnp.dot(own_pivot, gathered[0], preferred_element_type=jnp.float32)
    ).astype(jnp.bfloat16)
    folded = (
        lower_panel[:, :block_size].astype(jnp.float32)
        - jnp.dot(lower_panel[:, block_size:], lower_pivot, preferred_element_type=jnp.float32)
    ).astype(jnp.bfloat16)
    multipliers = jnp.concatenate([folded, lower_panel[:, block_size:]], 1)
    stacked = gathered.reshape(2 * block_size, col_count)
    col_index = lax.axis_index("pcol") * col_count + jnp.arange(col_count, dtype=jnp.int32)
    retained = col_index >= panel_width
    schur_rows = masked.astype(jnp.float32) - jnp.dot(
        multipliers, stacked, preferred_element_type=jnp.float32
    )
    schur_rows = jnp.where(retained[None, :], schur_rows, jnp.zeros_like(schur_rows))
    summed = lax.psum_scatter(
        schur_rows.astype(jnp.bfloat16), "layer", scatter_dimension=0, tiled=True
    ).astype(jnp.float32)
    ancestor = summed.reshape(1, 1, summed.shape[0], col_count)
    return (ancestor, lower_panel[None], upper_own[None])


def solution(mesh):
    placed = (
        P("layer", "prow", "pcol"),
        P("layer", None, "prow", "pcol"),
        P("layer", None, None, None),
        P("layer", "prow", "pcol"),
        P("layer", None, "pcol"),
    )
    return jax.shard_map(
        on_device,
        mesh=mesh,
        in_specs=placed,
        out_specs=(
            P("prow", "layer", None, "pcol"),
            P("layer", "prow", None),
            P("layer", "prow", "pcol"),
        ),
        check_vma=False,
    )
```

```python
import jax
import jax.numpy as jnp
from jax import lax
from jax.sharding import PartitionSpec as P


def ring(value, axis, size, step):
    return lax.ppermute(value, axis, [(i, (i + step) % size) for i in range(size)])


def gather_relative(value, axis, size):
    from_prev = ring(value, axis, size, 1)
    from_next = ring(value, axis, size, -1)
    half = value.shape[1] // 2
    far_lo = ring(from_prev[:, :half], axis, size, 1)
    far_hi = ring(from_next[:, half:], axis, size, -1)
    far = jnp.concatenate([far_lo, far_hi], 1)
    return jnp.concatenate([value, from_next, far, from_prev], 1)


def on_device(front, pivots, inverses, slab_pattern, pivot_pattern):
    block_size = inverses.shape[-1]
    panel_width = 2 * block_size
    row_count = front.shape[1]
    col_count = front.shape[2]
    own_rows = pivots.shape[2]
    masked = (
        front[0].reshape(row_count // block_size, block_size, col_count // block_size, block_size)
        * slab_pattern[0].astype(jnp.bfloat16)[:, None, :, None]
    ).reshape(row_count, col_count)
    pivot_masked = (
        pivots[0].reshape(2, own_rows, col_count // block_size, block_size)
        * pivot_pattern[0].astype(jnp.bfloat16)[:, None, :, None]
    ).reshape(2, own_rows, col_count)
    first_inverse = inverses[0, 0]
    second_inverse = inverses[0, 1]
    row_offset = lax.axis_index("prow") * own_rows
    pcol = lax.axis_index("pcol")
    n_prow = lax.axis_size("prow")
    n_pcol = lax.axis_size("pcol")
    assert n_prow == 4
    gathered = lax.all_gather(pivot_masked, "prow", axis=1, tiled=True)
    panel = jnp.roll(
        gather_relative(pivot_masked[:, :, :panel_width], "prow", n_prow), row_offset, axis=1
    )
    front_cols = masked[:, :panel_width]
    pivot_cols = panel[0]
    second_cols = panel[1]
    lower_pivot = jnp.dot(
        second_cols[:, :block_size], first_inverse, preferred_element_type=jnp.float32
    ).astype(jnp.bfloat16)
    lower_first = jnp.dot(
        front_cols[:, :block_size], first_inverse, preferred_element_type=jnp.float32
    ).astype(jnp.bfloat16)
    carried = (
        front_cols[:, block_size:].astype(jnp.float32)
        - jnp.dot(
            lower_first, pivot_cols[:, block_size:panel_width], preferred_element_type=jnp.float32
        )
    ).astype(jnp.bfloat16)
    lower_second = jnp.dot(carried, second_inverse, preferred_element_type=jnp.float32).astype(
        jnp.bfloat16
    )
    lower_panel = jnp.concatenate([lower_first, lower_second], 1)
    sent = lax.ppermute((lower_panel, lower_pivot), "pcol", [(0, i) for i in range(1, n_pcol)])
    on_root = pcol == 0
    lower_panel = jnp.where(on_root, lower_panel, sent[0])
    lower_pivot = jnp.where(on_root, lower_pivot, sent[1])
    own_pivot = lax.dynamic_slice_in_dim(lower_pivot, row_offset, own_rows, 0)
    upper_own = (
        pivot_masked[1].astype(jnp.float32)
        - jnp.dot(own_pivot, gathered[0], preferred_element_type=jnp.float32)
    ).astype(jnp.bfloat16)
    folded = (
        lower_panel[:, :block_size].astype(jnp.float32)
        - jnp.dot(lower_panel[:, block_size:], lower_pivot, preferred_element_type=jnp.float32)
    ).astype(jnp.bfloat16)
    multipliers = jnp.concatenate([folded, lower_panel[:, block_size:]], 1)
    stacked = gathered.reshape(2 * block_size, col_count)
    col_index = lax.axis_index("pcol") * col_count + jnp.arange(col_count, dtype=jnp.int32)
    retained = col_index >= panel_width
    schur_rows = masked.astype(jnp.float32) - jnp.dot(
        multipliers, stacked, preferred_element_type=jnp.float32
    )
    schur_rows = jnp.where(retained[None, :], schur_rows, jnp.zeros_like(schur_rows))
    side = 4
    by_y = [[x + side * y for y in range(side)] for x in range(side)]
    by_x = [[x + side * y for x in range(side)] for y in range(side)]
    partial = lax.psum_scatter(
        schur_rows.astype(jnp.bfloat16), "layer", scatter_dimension=0, tiled=True,
        axis_index_groups=by_y,
    )
    summed = lax.psum_scatter(
        partial.astype(jnp.float32), "layer", scatter_dimension=0, tiled=True,
        axis_index_groups=by_x,
    )
    ancestor = summed.reshape(1, 1, summed.shape[0], col_count)
    return (ancestor, lower_panel[None], upper_own[None])


def solution(mesh):
    placed = (
        P("layer", "prow", "pcol"),
        P("layer", None, "prow", "pcol"),
        P("layer", None, None, None),
        P("layer", "prow", "pcol"),
        P("layer", None, "pcol"),
    )
    return jax.shard_map(
        on_device,
        mesh=mesh,
        in_specs=placed,
        out_specs=(
            P("prow", "layer", None, "pcol"),
            P("layer", "prow", None),
            P("layer", "prow", "pcol"),
        ),
        check_vma=False,
    )
```

```python
import jax
import jax.numpy as jnp
from jax import lax
from jax.sharding import PartitionSpec as P


def ring(value, axis, size, step):
    return lax.ppermute(value, axis, [(i, (i + step) % size) for i in range(size)])


def gather_relative(value, axis, size):
    from_prev = ring(value, axis, size, 1)
    from_next = ring(value, axis, size, -1)
    half = value.shape[1] // 2
    far_lo = ring(from_prev[:, :half], axis, size, 1)
    far_hi = ring(from_next[:, half:], axis, size, -1)
    far = jnp.concatenate([far_lo, far_hi], 1)
    return jnp.concatenate([value, from_next, far, from_prev], 1)


def grid_shift(value, axis, side, dy, dx):
    pairs = []
    for y in range(side):
        for x in range(side):
            pairs.append((y * side + x, ((y + dy) % side) * side + (x + dx) % side))
    return lax.ppermute(value, axis, pairs)


def ring_reduce(blocks, send):
    half = blocks.shape[1] // 2
    far = blocks[2].astype(jnp.bfloat16)
    fwd1 = send(far[:half], 1)
    bwd1 = send(far[half:], -1)
    next_block = blocks[1]
    prev_block = blocks[3]
    fwd2 = send(
        jnp.concatenate([next_block[:half] + fwd1.astype(jnp.float32), next_block[half:]], 0).astype(
            jnp.bfloat16
        ),
        1,
    )
    bwd2 = send(
        jnp.concatenate([prev_block[:half], prev_block[half:] + bwd1.astype(jnp.float32)], 0).astype(
            jnp.bfloat16
        ),
        -1,
    )
    return blocks[0] + fwd2.astype(jnp.float32) + bwd2.astype(jnp.float32)


def relative(value, own, axis):
    return jnp.stack(
        [lax.dynamic_index_in_dim(value, (own + j) % 4, axis, keepdims=False) for j in range(4)], 0
    )


def grid_reduce_scatter(schur, axis):
    side = 4
    index = lax.axis_index(axis)
    gy = index // side
    gx = index % side
    rows, width = schur.shape
    part = rows // (side * side)
    grid = schur.reshape(side, side, part, width)
    left = grid[..., : width // 2]
    right = grid[..., width // 2 :]

    def along_x(v, step):
        return grid_shift(v, axis, side, 0, step)

    def along_y(v, step):
        return grid_shift(v, axis, side, step, 0)

    left = ring_reduce(relative(left, gx, 1), along_x)
    left = ring_reduce(relative(left, gy, 0), along_y)
    right = ring_reduce(relative(right, gy, 0), along_y)
    right = ring_reduce(relative(right, gx, 0), along_x)
    return jnp.concatenate([left, right], 1)


def on_device(front, pivots, inverses, slab_pattern, pivot_pattern):
    block_size = inverses.shape[-1]
    panel_width = 2 * block_size
    row_count = front.shape[1]
    col_count = front.shape[2]
    own_rows = pivots.shape[2]
    masked = (
        front[0].reshape(row_count // block_size, block_size, col_count // block_size, block_size)
        * slab_pattern[0].astype(jnp.bfloat16)[:, None, :, None]
    ).reshape(row_count, col_count)
    pivot_masked = (
        pivots[0].reshape(2, own_rows, col_count // block_size, block_size)
        * pivot_pattern[0].astype(jnp.bfloat16)[:, None, :, None]
    ).reshape(2, own_rows, col_count)
    first_inverse = inverses[0, 0]
    second_inverse = inverses[0, 1]
    row_offset = lax.axis_index("prow") * own_rows
    pcol = lax.axis_index("pcol")
    n_prow = lax.axis_size("prow")
    n_pcol = lax.axis_size("pcol")
    assert n_prow == 4
    half = col_count // 2
    first_half = pivot_masked[:, :, :half]
    gathered = lax.all_gather(first_half, "prow", axis=1, tiled=True)
    second_half, gathered = lax.optimization_barrier((pivot_masked[:, :, half:], gathered))
    gathered_rel = gather_relative(second_half, "prow", n_prow)
    panel = jnp.roll(
        gather_relative(pivot_masked[:, :, :panel_width], "prow", n_prow), row_offset, axis=1
    )
    front_cols = masked[:, :panel_width]
    pivot_cols = panel[0]
    second_cols = panel[1]
    lower_pivot = jnp.dot(
        second_cols[:, :block_size], first_inverse, preferred_element_type=jnp.float32
    ).astype(jnp.bfloat16)
    lower_first = jnp.dot(
        front_cols[:, :block_size], first_inverse, preferred_element_type=jnp.float32
    ).astype(jnp.bfloat16)
    carried = (
        front_cols[:, block_size:].astype(jnp.float32)
        - jnp.dot(
            lower_first, pivot_cols[:, block_size:panel_width], preferred_element_type=jnp.float32
        )
    ).astype(jnp.bfloat16)
    lower_second = jnp.dot(carried, second_inverse, preferred_element_type=jnp.float32).astype(
        jnp.bfloat16
    )
    lower_panel = jnp.concatenate([lower_first, lower_second], 1)
    sent = lax.ppermute((lower_panel, lower_pivot), "pcol", [(0, i) for i in range(1, n_pcol)])
    on_root = pcol == 0
    lower_panel = jnp.where(on_root, lower_panel, sent[0])
    lower_pivot = jnp.where(on_root, lower_pivot, sent[1])
    own_pivot = lax.dynamic_slice_in_dim(lower_pivot, row_offset, own_rows, 0)
    upper_own = jnp.concatenate(
        [
            jnp.dot(own_pivot, gathered[0], preferred_element_type=jnp.float32),
            jnp.dot(
                jnp.roll(own_pivot, -row_offset, axis=1),
                gathered_rel[0],
                preferred_element_type=jnp.float32,
            ),
        ],
        1,
    )
    upper_own = (pivot_masked[1].astype(jnp.float32) - upper_own).astype(jnp.bfloat16)
    folded = (
        lower_panel[:, :block_size].astype(jnp.float32)
        - jnp.dot(lower_panel[:, block_size:], lower_pivot, preferred_element_type=jnp.float32)
    ).astype(jnp.bfloat16)
    multipliers = jnp.concatenate([folded, lower_panel[:, block_size:]], 1)
    multipliers_rel = jnp.concatenate(
        [
            jnp.roll(folded, -row_offset, axis=1),
            jnp.roll(lower_panel[:, block_size:], -row_offset, axis=1),
        ],
        1,
    )
    col_index = pcol * col_count + jnp.arange(col_count, dtype=jnp.int32)
    retained = col_index >= panel_width
    schur_first = masked[:, :half].astype(jnp.float32) - jnp.dot(
        multipliers, gathered.reshape(2 * block_size, half), preferred_element_type=jnp.float32
    )
    schur_first = jnp.where(retained[None, :half], schur_first, jnp.zeros_like(schur_first))
    summed_first = lax.psum_scatter(
        schur_first.astype(jnp.bfloat16), "layer", scatter_dimension=0, tiled=True
    ).astype(jnp.float32)
    schur_second = masked[:, half:].astype(jnp.float32) - jnp.dot(
        multipliers_rel,
        gathered_rel.reshape(2 * block_size, half),
        preferred_element_type=jnp.float32,
    )
    schur_second = jnp.where(retained[None, half:], schur_second, jnp.zeros_like(schur_second))
    summed = jnp.concatenate([summed_first, grid_reduce_scatter(schur_second, "layer")], 1)
    ancestor = summed.reshape(1, 1, summed.shape[0], col_count)
    return (ancestor, lower_panel[None], upper_own[None])


def solution(mesh):
    placed = (
        P("layer", "prow", "pcol"),
        P("layer", None, "prow", "pcol"),
        P("layer", None, None, None),
        P("layer", "prow", "pcol"),
        P("layer", None, "pcol"),
    )
    return jax.shard_map(
        on_device,
        mesh=mesh,
        in_specs=placed,
        out_specs=(
            P("prow", "layer", None, "pcol"),
            P("layer", "prow", None),
            P("layer", "prow", "pcol"),
        ),
        check_vma=False,
    )
```

```python
import jax
import jax.numpy as jnp
from jax import lax
from jax.sharding import PartitionSpec as P


def ring(value, axis, size, step):
    return lax.ppermute(value, axis, [(i, (i + step) % size) for i in range(size)])


def gather_relative(value, axis, size):
    from_prev = ring(value, axis, size, 1)
    from_next = ring(value, axis, size, -1)
    half = value.shape[1] // 2
    far_lo = ring(from_prev[:, :half], axis, size, 1)
    far_hi = ring(from_next[:, half:], axis, size, -1)
    far = jnp.concatenate([far_lo, far_hi], 1)
    return jnp.concatenate([value, from_next, far, from_prev], 1)


def grid_shift(value, axis, side, dy, dx):
    pairs = []
    for y in range(side):
        for x in range(side):
            pairs.append((y * side + x, ((y + dy) % side) * side + (x + dx) % side))
    return lax.ppermute(value, axis, pairs)


def ring_reduce(blocks, send):
    half = blocks.shape[1] // 2
    far = blocks[2].astype(jnp.bfloat16)
    fwd1 = send(far[:half], 1)
    bwd1 = send(far[half:], -1)
    next_block = blocks[1]
    prev_block = blocks[3]
    fwd2 = send(
        jnp.concatenate([next_block[:half] + fwd1.astype(jnp.float32), next_block[half:]], 0).astype(
            jnp.bfloat16
        ),
        1,
    )
    bwd2 = send(
        jnp.concatenate([prev_block[:half], prev_block[half:] + bwd1.astype(jnp.float32)], 0).astype(
            jnp.bfloat16
        ),
        -1,
    )
    return blocks[0] + fwd2.astype(jnp.float32) + bwd2.astype(jnp.float32)


def relative(value, own, axis):
    return jnp.stack(
        [lax.dynamic_index_in_dim(value, (own + j) % 4, axis, keepdims=False) for j in range(4)], 0
    )


def grid_reduce_scatter(schur, axis):
    side = 4
    index = lax.axis_index(axis)
    gy = index // side
    gx = index % side
    rows, width = schur.shape
    part = rows // (side * side)
    grid = schur.reshape(side, side, part, width)
    left = grid[..., : width // 2]
    right = grid[..., width // 2 :]

    def along_x(v, step):
        return grid_shift(v, axis, side, 0, step)

    def along_y(v, step):
        return grid_shift(v, axis, side, step, 0)

    left = ring_reduce(relative(left, gx, 1), along_x)
    left = ring_reduce(relative(left, gy, 0), along_y)
    right = ring_reduce(relative(right, gy, 0), along_y)
    right = ring_reduce(relative(right, gx, 0), along_x)
    return jnp.concatenate([left, right], 1)


def on_device(front, pivots, inverses, slab_pattern, pivot_pattern):
    block_size = inverses.shape[-1]
    panel_width = 2 * block_size
    row_count = front.shape[1]
    col_count = front.shape[2]
    own_rows = pivots.shape[2]
    masked = (
        front[0].reshape(row_count // block_size, block_size, col_count // block_size, block_size)
        * slab_pattern[0].astype(jnp.bfloat16)[:, None, :, None]
    ).reshape(row_count, col_count)
    pivot_masked = (
        pivots[0].reshape(2, own_rows, col_count // block_size, block_size)
        * pivot_pattern[0].astype(jnp.bfloat16)[:, None, :, None]
    ).reshape(2, own_rows, col_count)
    first_inverse = inverses[0, 0]
    second_inverse = inverses[0, 1]
    row_offset = lax.axis_index("prow") * own_rows
    pcol = lax.axis_index("pcol")
    n_prow = lax.axis_size("prow")
    n_pcol = lax.axis_size("pcol")
    assert n_prow == 4
    half = (col_count * 11 // 16) // block_size * block_size
    gathered = lax.all_gather(pivot_masked[:, :, :half], "prow", axis=1, tiled=True)
    panel = jnp.roll(
        gather_relative(pivot_masked[:, :, :panel_width], "prow", n_prow), row_offset, axis=1
    )
    front_cols = masked[:, :panel_width]
    pivot_cols = panel[0]
    second_cols = panel[1]
    lower_pivot = jnp.dot(
        second_cols[:, :block_size], first_inverse, preferred_element_type=jnp.float32
    ).astype(jnp.bfloat16)
    lower_first = jnp.dot(
        front_cols[:, :block_size], first_inverse, preferred_element_type=jnp.float32
    ).astype(jnp.bfloat16)
    carried = (
        front_cols[:, block_size:].astype(jnp.float32)
        - jnp.dot(
            lower_first, pivot_cols[:, block_size:panel_width], preferred_element_type=jnp.float32
        )
    ).astype(jnp.bfloat16)
    lower_second = jnp.dot(carried, second_inverse, preferred_element_type=jnp.float32).astype(
        jnp.bfloat16
    )
    lower_panel = jnp.concatenate([lower_first, lower_second], 1)
    sent = lax.ppermute((lower_panel, lower_pivot), "pcol", [(0, i) for i in range(1, n_pcol)])
    on_root = pcol == 0
    lower_panel = jnp.where(on_root, lower_panel, sent[0])
    lower_pivot = jnp.where(on_root, lower_pivot, sent[1])
    folded = (
        lower_panel[:, :block_size].astype(jnp.float32)
        - jnp.dot(lower_panel[:, block_size:], lower_pivot, preferred_element_type=jnp.float32)
    ).astype(jnp.bfloat16)
    multipliers = jnp.concatenate([folded, lower_panel[:, block_size:]], 1)
    multipliers_rel = jnp.concatenate(
        [
            jnp.roll(folded, -row_offset, axis=1),
            jnp.roll(lower_panel[:, block_size:], -row_offset, axis=1),
        ],
        1,
    )
    col_index = pcol * col_count + jnp.arange(col_count, dtype=jnp.int32)
    retained = col_index >= panel_width
    schur_first = masked[:, :half].astype(jnp.float32) - jnp.dot(
        multipliers, gathered.reshape(2 * block_size, half), preferred_element_type=jnp.float32
    )
    schur_first = jnp.where(retained[None, :half], schur_first, jnp.zeros_like(schur_first))
    second_half, schur_first = lax.optimization_barrier(
        (pivot_masked[:, :, half:], schur_first.astype(jnp.bfloat16))
    )
    summed_first = lax.psum_scatter(
        schur_first, "layer", scatter_dimension=0, tiled=True
    ).astype(jnp.float32)
    gathered_rel = gather_relative(second_half, "prow", n_prow)
    own_pivot = lax.dynamic_slice_in_dim(lower_pivot, row_offset, own_rows, 0)
    upper_own = jnp.concatenate(
        [
            jnp.dot(own_pivot, gathered[0], preferred_element_type=jnp.float32),
            jnp.dot(
                jnp.roll(own_pivot, -row_offset, axis=1),
                gathered_rel[0],
                preferred_element_type=jnp.float32,
            ),
        ],
        1,
    )
    upper_own = (pivot_masked[1].astype(jnp.float32) - upper_own).astype(jnp.bfloat16)
    schur_second = masked[:, half:].astype(jnp.float32) - jnp.dot(
        multipliers_rel,
        gathered_rel.reshape(2 * block_size, col_count - half),
        preferred_element_type=jnp.float32,
    )
    schur_second = jnp.where(retained[None, half:], schur_second, jnp.zeros_like(schur_second))
    summed = jnp.concatenate([summed_first, grid_reduce_scatter(schur_second, "layer")], 1)
    ancestor = summed.reshape(1, 1, summed.shape[0], col_count)
    return (ancestor, lower_panel[None], upper_own[None])


def solution(mesh):
    placed = (
        P("layer", "prow", "pcol"),
        P("layer", None, "prow", "pcol"),
        P("layer", None, None, None),
        P("layer", "prow", "pcol"),
        P("layer", None, "pcol"),
    )
    return jax.shard_map(
        on_device,
        mesh=mesh,
        in_specs=placed,
        out_specs=(
            P("prow", "layer", None, "pcol"),
            P("layer", "prow", None),
            P("layer", "prow", "pcol"),
        ),
        check_vma=False,
    )
```

```python
import jax
import jax.numpy as jnp
from jax import lax
from jax.sharding import PartitionSpec as P

SC_SHARE = 8
PIECES = 2


def ring(value, axis, size, step):
    return lax.ppermute(value, axis, [(i, (i + step) % size) for i in range(size)])


def gather_relative(value, axis, size):
    from_prev = ring(value, axis, size, 1)
    from_next = ring(value, axis, size, -1)
    half = value.shape[1] // 2
    far_lo = ring(from_prev[:, :half], axis, size, 1)
    far_hi = ring(from_next[:, half:], axis, size, -1)
    far = jnp.concatenate([far_lo, far_hi], 1)
    return jnp.concatenate([value, from_next, far, from_prev], 1)


def grid_shift(value, axis, side, dy, dx):
    pairs = []
    for y in range(side):
        for x in range(side):
            pairs.append((y * side + x, ((y + dy) % side) * side + (x + dx) % side))
    return lax.ppermute(value, axis, pairs)


def ring_reduce(blocks, send):
    half = blocks.shape[1] // 2
    far = blocks[2].astype(jnp.bfloat16)
    fwd1 = send(far[:half], 1)
    bwd1 = send(far[half:], -1)
    next_block = blocks[1]
    prev_block = blocks[3]
    fwd2 = send(
        jnp.concatenate([next_block[:half] + fwd1.astype(jnp.float32), next_block[half:]], 0).astype(
            jnp.bfloat16
        ),
        1,
    )
    bwd2 = send(
        jnp.concatenate([prev_block[:half], prev_block[half:] + bwd1.astype(jnp.float32)], 0).astype(
            jnp.bfloat16
        ),
        -1,
    )
    return blocks[0] + fwd2.astype(jnp.float32) + bwd2.astype(jnp.float32)


def relative(value, own, axis):
    return jnp.stack(
        [lax.dynamic_index_in_dim(value, (own + j) % 4, axis, keepdims=False) for j in range(4)], 0
    )


def grid_reduce_scatter(schur, axis):
    side = 4
    index = lax.axis_index(axis)
    gy = index // side
    gx = index % side
    rows, width = schur.shape
    part = rows // (side * side)
    grid = schur.reshape(side, side, part, width)
    left = grid[..., : width // 2]
    right = grid[..., width // 2 :]

    def along_x(v, step):
        return grid_shift(v, axis, side, 0, step)

    def along_y(v, step):
        return grid_shift(v, axis, side, step, 0)

    left = ring_reduce(relative(left, gx, 1), along_x)
    left = ring_reduce(relative(left, gy, 0), along_y)
    right = ring_reduce(relative(right, gy, 0), along_y)
    right = ring_reduce(relative(right, gx, 0), along_x)
    return jnp.concatenate([left, right], 1)


def on_device(front, pivots, inverses, slab_pattern, pivot_pattern):
    block_size = inverses.shape[-1]
    panel_width = 2 * block_size
    row_count = front.shape[1]
    col_count = front.shape[2]
    own_rows = pivots.shape[2]
    masked = (
        front[0].reshape(row_count // block_size, block_size, col_count // block_size, block_size)
        * slab_pattern[0].astype(jnp.bfloat16)[:, None, :, None]
    ).reshape(row_count, col_count)
    pivot_masked = (
        pivots[0].reshape(2, own_rows, col_count // block_size, block_size)
        * pivot_pattern[0].astype(jnp.bfloat16)[:, None, :, None]
    ).reshape(2, own_rows, col_count)
    first_inverse = inverses[0, 0]
    second_inverse = inverses[0, 1]
    row_offset = lax.axis_index("prow") * own_rows
    pcol = lax.axis_index("pcol")
    n_prow = lax.axis_size("prow")
    n_pcol = lax.axis_size("pcol")
    assert n_prow == 4
    half = (col_count * SC_SHARE // 16) // block_size * block_size
    gathered = lax.all_gather(pivot_masked[:, :, :half], "prow", axis=1, tiled=True)
    panel = jnp.roll(
        gather_relative(pivot_masked[:, :, :panel_width], "prow", n_prow), row_offset, axis=1
    )
    front_cols = masked[:, :panel_width]
    pivot_cols = panel[0]
    second_cols = panel[1]
    lower_pivot = jnp.dot(
        second_cols[:, :block_size], first_inverse, preferred_element_type=jnp.float32
    ).astype(jnp.bfloat16)
    lower_first = jnp.dot(
        front_cols[:, :block_size], first_inverse, preferred_element_type=jnp.float32
    ).astype(jnp.bfloat16)
    carried = (
        front_cols[:, block_size:].astype(jnp.float32)
        - jnp.dot(
            lower_first, pivot_cols[:, block_size:panel_width], preferred_element_type=jnp.float32
        )
    ).astype(jnp.bfloat16)
    lower_second = jnp.dot(carried, second_inverse, preferred_element_type=jnp.float32).astype(
        jnp.bfloat16
    )
    lower_panel = jnp.concatenate([lower_first, lower_second], 1)
    sent = lax.ppermute((lower_panel, lower_pivot), "pcol", [(0, i) for i in range(1, n_pcol)])
    on_root = pcol == 0
    lower_panel = jnp.where(on_root, lower_panel, sent[0])
    lower_pivot = jnp.where(on_root, lower_pivot, sent[1])
    folded = (
        lower_panel[:, :block_size].astype(jnp.float32)
        - jnp.dot(lower_panel[:, block_size:], lower_pivot, preferred_element_type=jnp.float32)
    ).astype(jnp.bfloat16)
    multipliers = jnp.concatenate([folded, lower_panel[:, block_size:]], 1)
    multipliers_rel = jnp.concatenate(
        [
            jnp.roll(folded, -row_offset, axis=1),
            jnp.roll(lower_panel[:, block_size:], -row_offset, axis=1),
        ],
        1,
    )
    col_index = pcol * col_count + jnp.arange(col_count, dtype=jnp.int32)
    retained = col_index >= panel_width
    schur_first = masked[:, :half].astype(jnp.float32) - jnp.dot(
        multipliers, gathered.reshape(2 * block_size, half), preferred_element_type=jnp.float32
    )
    schur_first = jnp.where(retained[None, :half], schur_first, jnp.zeros_like(schur_first))
    pending, schur_first = lax.optimization_barrier(
        (pivot_masked[:, :, half:], schur_first.astype(jnp.bfloat16))
    )
    summed_parts = [
        lax.psum_scatter(schur_first, "layer", scatter_dimension=0, tiled=True).astype(jnp.float32)
    ]
    own_pivot = lax.dynamic_slice_in_dim(lower_pivot, row_offset, own_rows, 0)
    upper_parts = [jnp.dot(own_pivot, gathered[0], preferred_element_type=jnp.float32)]
    piece = (col_count - half) // PIECES
    for k in range(PIECES):
        start = half + k * piece
        gathered_rel = gather_relative(pending[:, :, :piece], "prow", n_prow)
        if k + 1 < PIECES:
            pending, gathered_rel = lax.optimization_barrier((pending[:, :, piece:], gathered_rel))
        upper_parts.append(
            jnp.dot(
                jnp.roll(own_pivot, -row_offset, axis=1),
                gathered_rel[0],
                preferred_element_type=jnp.float32,
            )
        )
        schur_part = masked[:, start : start + piece].astype(jnp.float32) - jnp.dot(
            multipliers_rel,
            gathered_rel.reshape(2 * block_size, piece),
            preferred_element_type=jnp.float32,
        )
        schur_part = jnp.where(
            retained[None, start : start + piece], schur_part, jnp.zeros_like(schur_part)
        )
        summed_parts.append(grid_reduce_scatter(schur_part, "layer"))
    upper_own = jnp.concatenate(upper_parts, 1)
    upper_own = (pivot_masked[1].astype(jnp.float32) - upper_own).astype(jnp.bfloat16)
    summed = jnp.concatenate(summed_parts, 1)
    ancestor = summed.reshape(1, 1, summed.shape[0], col_count)
    return (ancestor, lower_panel[None], upper_own[None])


def solution(mesh):
    placed = (
        P("layer", "prow", "pcol"),
        P("layer", None, "prow", "pcol"),
        P("layer", None, None, None),
        P("layer", "prow", "pcol"),
        P("layer", None, "pcol"),
    )
    return jax.shard_map(
        on_device,
        mesh=mesh,
        in_specs=placed,
        out_specs=(
            P("prow", "layer", None, "pcol"),
            P("layer", "prow", None),
            P("layer", "prow", "pcol"),
        ),
        check_vma=False,
    )
```

```python
import jax
import jax.numpy as jnp
from jax import lax
from jax.sharding import PartitionSpec as P


def ring(value, axis, size, step):
    return lax.ppermute(value, axis, [(i, (i + step) % size) for i in range(size)])


def gather_relative(value, axis, size):
    from_prev = ring(value, axis, size, 1)
    from_next = ring(value, axis, size, -1)
    half = value.shape[1] // 2
    far_lo = ring(from_prev[:, :half], axis, size, 1)
    far_hi = ring(from_next[:, half:], axis, size, -1)
    far = jnp.concatenate([far_lo, far_hi], 1)
    return jnp.concatenate([value, from_next, far, from_prev], 1)


def grid_shift(value, axis, side, dy, dx):
    pairs = []
    for y in range(side):
        for x in range(side):
            pairs.append((y * side + x, ((y + dy) % side) * side + (x + dx) % side))
    return lax.ppermute(value, axis, pairs)


def ring_reduce(blocks, send):
    half = blocks.shape[1] // 2
    far = blocks[2].astype(jnp.bfloat16)
    fwd1 = send(far[:half], 1)
    bwd1 = send(far[half:], -1)
    next_block = blocks[1]
    prev_block = blocks[3]
    fwd2 = send(
        jnp.concatenate([next_block[:half] + fwd1.astype(jnp.float32), next_block[half:]], 0).astype(
            jnp.bfloat16
        ),
        1,
    )
    bwd2 = send(
        jnp.concatenate([prev_block[:half], prev_block[half:] + bwd1.astype(jnp.float32)], 0).astype(
            jnp.bfloat16
        ),
        -1,
    )
    return blocks[0] + fwd2.astype(jnp.float32) + bwd2.astype(jnp.float32)


def relative(value, own, axis):
    return jnp.stack(
        [lax.dynamic_index_in_dim(value, (own + j) % 4, axis, keepdims=False) for j in range(4)], 0
    )


def grid_reduce_scatter(schur, axis):
    side = 4
    index = lax.axis_index(axis)
    gy = index // side
    gx = index % side
    rows, width = schur.shape
    part = rows // (side * side)
    grid = schur.reshape(side, side, part, width)
    left = grid[..., : width // 2]
    right = grid[..., width // 2 :]

    def along_x(v, step):
        return grid_shift(v, axis, side, 0, step)

    def along_y(v, step):
        return grid_shift(v, axis, side, step, 0)

    left = ring_reduce(relative(left, gx, 1), along_x)
    left = ring_reduce(relative(left, gy, 0), along_y)
    right = ring_reduce(relative(right, gy, 0), along_y)
    right = ring_reduce(relative(right, gx, 0), along_x)
    return jnp.concatenate([left, right], 1)


def on_device(front, pivots, inverses, slab_pattern, pivot_pattern):
    block_size = inverses.shape[-1]
    panel_width = 2 * block_size
    row_count = front.shape[1]
    col_count = front.shape[2]
    own_rows = pivots.shape[2]
    masked = (
        front[0].reshape(row_count // block_size, block_size, col_count // block_size, block_size)
        * slab_pattern[0].astype(jnp.bfloat16)[:, None, :, None]
    ).reshape(row_count, col_count)
    pivot_masked = (
        pivots[0].reshape(2, own_rows, col_count // block_size, block_size)
        * pivot_pattern[0].astype(jnp.bfloat16)[:, None, :, None]
    ).reshape(2, own_rows, col_count)
    first_inverse = inverses[0, 0]
    second_inverse = inverses[0, 1]
    row_offset = lax.axis_index("prow") * own_rows
    pcol = lax.axis_index("pcol")
    n_prow = lax.axis_size("prow")
    n_pcol = lax.axis_size("pcol")
    assert n_prow == 4
    half = (col_count * 11 // 16) // block_size * block_size
    gathered = lax.all_gather(pivot_masked[:, :, :half], "prow", axis=1, tiled=True)
    later_cols, gathered = lax.optimization_barrier((pivot_masked[:, :, half:], gathered))
    panel = jnp.roll(
        gather_relative(pivot_masked[:, :, :panel_width], "prow", n_prow), row_offset, axis=1
    )
    front_cols = masked[:, :panel_width]
    pivot_cols = panel[0]
    second_cols = panel[1]
    lower_pivot = jnp.dot(
        second_cols[:, :block_size], first_inverse, preferred_element_type=jnp.float32
    ).astype(jnp.bfloat16)
    lower_first = jnp.dot(
        front_cols[:, :block_size], first_inverse, preferred_element_type=jnp.float32
    ).astype(jnp.bfloat16)
    carried = (
        front_cols[:, block_size:].astype(jnp.float32)
        - jnp.dot(
            lower_first, pivot_cols[:, block_size:panel_width], preferred_element_type=jnp.float32
        )
    ).astype(jnp.bfloat16)
    lower_second = jnp.dot(carried, second_inverse, preferred_element_type=jnp.float32).astype(
        jnp.bfloat16
    )
    lower_panel = jnp.concatenate([lower_first, lower_second], 1)
    sent = lax.ppermute((lower_panel, lower_pivot), "pcol", [(0, i) for i in range(1, n_pcol)])
    on_root = pcol == 0
    lower_panel = jnp.where(on_root, lower_panel, sent[0])
    lower_pivot = jnp.where(on_root, lower_pivot, sent[1])
    folded = (
        lower_panel[:, :block_size].astype(jnp.float32)
        - jnp.dot(lower_panel[:, block_size:], lower_pivot, preferred_element_type=jnp.float32)
    ).astype(jnp.bfloat16)
    multipliers = jnp.concatenate([folded, lower_panel[:, block_size:]], 1)
    multipliers_rel = jnp.concatenate(
        [
            jnp.roll(folded, -row_offset, axis=1),
            jnp.roll(lower_panel[:, block_size:], -row_offset, axis=1),
        ],
        1,
    )
    col_index = pcol * col_count + jnp.arange(col_count, dtype=jnp.int32)
    retained = col_index >= panel_width
    schur_first = masked[:, :half].astype(jnp.float32) - jnp.dot(
        multipliers, gathered.reshape(2 * block_size, half), preferred_element_type=jnp.float32
    )
    schur_first = jnp.where(retained[None, :half], schur_first, jnp.zeros_like(schur_first))
    second_half, schur_first = lax.optimization_barrier(
        (later_cols, schur_first.astype(jnp.bfloat16))
    )
    summed_first = lax.psum_scatter(
        schur_first, "layer", scatter_dimension=0, tiled=True
    ).astype(jnp.float32)
    gathered_rel = gather_relative(second_half, "prow", n_prow)
    own_pivot = lax.dynamic_slice_in_dim(lower_pivot, row_offset, own_rows, 0)
    upper_own = jnp.concatenate(
        [
            (
                pivot_masked[1, :, :half].astype(jnp.float32)
                - jnp.dot(own_pivot, gathered[0], preferred_element_type=jnp.float32)
            ).astype(jnp.bfloat16),
            (
                pivot_masked[1, :, half:].astype(jnp.float32)
                - jnp.dot(
                    jnp.roll(own_pivot, -row_offset, axis=1),
                    gathered_rel[0],
                    preferred_element_type=jnp.float32,
                )
            ).astype(jnp.bfloat16),
        ],
        1,
    )
    schur_second = masked[:, half:].astype(jnp.float32) - jnp.dot(
        multipliers_rel,
        gathered_rel.reshape(2 * block_size, col_count - half),
        preferred_element_type=jnp.float32,
    )
    schur_second = jnp.where(retained[None, half:], schur_second, jnp.zeros_like(schur_second))
    summed = jnp.concatenate([summed_first, grid_reduce_scatter(schur_second, "layer")], 1)
    ancestor = summed.reshape(1, 1, summed.shape[0], col_count)
    return (ancestor, lower_panel[None], upper_own[None])


def solution(mesh):
    placed = (
        P("layer", "prow", "pcol"),
        P("layer", None, "prow", "pcol"),
        P("layer", None, None, None),
        P("layer", "prow", "pcol"),
        P("layer", None, "pcol"),
    )
    return jax.shard_map(
        on_device,
        mesh=mesh,
        in_specs=placed,
        out_specs=(
            P("prow", "layer", None, "pcol"),
            P("layer", "prow", None),
            P("layer", "prow", "pcol"),
        ),
        check_vma=False,
    )
```

```python
import jax
import jax.numpy as jnp
from jax import lax
from jax.sharding import PartitionSpec as P


def ring(value, axis, size, step):
    return lax.ppermute(value, axis, [(i, (i + step) % size) for i in range(size)])


def gather_relative(value, axis, size):
    from_prev = ring(value, axis, size, 1)
    from_next = ring(value, axis, size, -1)
    half = value.shape[1] // 2
    far_lo = ring(from_prev[:, :half], axis, size, 1)
    far_hi = ring(from_next[:, half:], axis, size, -1)
    far = jnp.concatenate([far_lo, far_hi], 1)
    return jnp.concatenate([value, from_next, far, from_prev], 1)


def grid_shift(value, axis, side, dy, dx):
    pairs = []
    for y in range(side):
        for x in range(side):
            pairs.append((y * side + x, ((y + dy) % side) * side + (x + dx) % side))
    return lax.ppermute(value, axis, pairs)


def ring_reduce(blocks, send):
    half = blocks.shape[1] // 2
    far = blocks[2].astype(jnp.bfloat16)
    fwd1 = send(far[:half], 1)
    bwd1 = send(far[half:], -1)
    next_block = blocks[1]
    prev_block = blocks[3]
    fwd2 = send(
        jnp.concatenate([next_block[:half] + fwd1.astype(jnp.float32), next_block[half:]], 0).astype(
            jnp.bfloat16
        ),
        1,
    )
    bwd2 = send(
        jnp.concatenate([prev_block[:half], prev_block[half:] + bwd1.astype(jnp.float32)], 0).astype(
            jnp.bfloat16
        ),
        -1,
    )
    return blocks[0] + fwd2.astype(jnp.float32) + bwd2.astype(jnp.float32)


def relative(value, own, axis):
    return jnp.stack(
        [lax.dynamic_index_in_dim(value, (own + j) % 4, axis, keepdims=False) for j in range(4)], 0
    )


def grid_reduce_scatter(schur, axis):
    side = 4
    index = lax.axis_index(axis)
    gy = index // side
    gx = index % side
    rows, width = schur.shape
    part = rows // (side * side)
    grid = schur.reshape(side, side, part, width)
    left = grid[..., : width // 2]
    right = grid[..., width // 2 :]

    def along_x(v, step):
        return grid_shift(v, axis, side, 0, step)

    def along_y(v, step):
        return grid_shift(v, axis, side, step, 0)

    left = ring_reduce(relative(left, gx, 1), along_x)
    left = ring_reduce(relative(left, gy, 0), along_y)
    right = ring_reduce(relative(right, gy, 0), along_y)
    right = ring_reduce(relative(right, gx, 0), along_x)
    return jnp.concatenate([left, right], 1)


def on_device(front, pivots, inverses, slab_pattern, pivot_pattern):
    block_size = inverses.shape[-1]
    panel_width = 2 * block_size
    row_count = front.shape[1]
    col_count = front.shape[2]
    own_rows = pivots.shape[2]
    masked = (
        front[0].reshape(row_count // block_size, block_size, col_count // block_size, block_size)
        * slab_pattern[0].astype(jnp.bfloat16)[:, None, :, None]
    ).reshape(row_count, col_count)
    pivot_masked = (
        pivots[0].reshape(2, own_rows, col_count // block_size, block_size)
        * pivot_pattern[0].astype(jnp.bfloat16)[:, None, :, None]
    ).reshape(2, own_rows, col_count)
    first_inverse = inverses[0, 0]
    second_inverse = inverses[0, 1]
    row_offset = lax.axis_index("prow") * own_rows
    pcol = lax.axis_index("pcol")
    n_prow = lax.axis_size("prow")
    n_pcol = lax.axis_size("pcol")
    assert n_prow == 4
    half = (col_count * 10 // 16) // block_size * block_size
    gathered = lax.all_gather(pivot_masked[:, :, :half], "prow", axis=1, tiled=True)
    later_cols, gathered = lax.optimization_barrier((pivot_masked[:, :, half:], gathered))
    panel = jnp.roll(
        gather_relative(pivot_masked[:, :, :panel_width], "prow", n_prow), row_offset, axis=1
    )
    front_cols = masked[:, :panel_width]
    pivot_cols = panel[0]
    second_cols = panel[1]
    lower_pivot = jnp.dot(
        second_cols[:, :block_size], first_inverse, preferred_element_type=jnp.float32
    ).astype(jnp.bfloat16)
    lower_first = jnp.dot(
        front_cols[:, :block_size], first_inverse, preferred_element_type=jnp.float32
    ).astype(jnp.bfloat16)
    carried = (
        front_cols[:, block_size:].astype(jnp.float32)
        - jnp.dot(
            lower_first, pivot_cols[:, block_size:panel_width], preferred_element_type=jnp.float32
        )
    ).astype(jnp.bfloat16)
    lower_second = jnp.dot(carried, second_inverse, preferred_element_type=jnp.float32).astype(
        jnp.bfloat16
    )
    lower_panel = jnp.concatenate([lower_first, lower_second], 1)
    sent = lax.ppermute((lower_panel, lower_pivot), "pcol", [(0, i) for i in range(1, n_pcol)])
    on_root = pcol == 0
    lower_panel = jnp.where(on_root, lower_panel, sent[0])
    lower_pivot = jnp.where(on_root, lower_pivot, sent[1])
    folded = (
        lower_panel[:, :block_size].astype(jnp.float32)
        - jnp.dot(lower_panel[:, block_size:], lower_pivot, preferred_element_type=jnp.float32)
    ).astype(jnp.bfloat16)
    multipliers = jnp.concatenate([folded, lower_panel[:, block_size:]], 1)
    multipliers_rel = jnp.concatenate(
        [
            jnp.roll(folded, -row_offset, axis=1),
            jnp.roll(lower_panel[:, block_size:], -row_offset, axis=1),
        ],
        1,
    )
    col_index = pcol * col_count + jnp.arange(col_count, dtype=jnp.int32)
    retained = col_index >= panel_width
    schur_first = masked[:, :half].astype(jnp.float32) - jnp.dot(
        multipliers, gathered.reshape(2 * block_size, half), preferred_element_type=jnp.float32
    )
    schur_first = jnp.where(retained[None, :half], schur_first, jnp.zeros_like(schur_first))
    second_half, schur_first = lax.optimization_barrier(
        (later_cols, schur_first.astype(jnp.bfloat16))
    )
    summed_first = lax.psum_scatter(
        schur_first, "layer", scatter_dimension=0, tiled=True
    ).astype(jnp.float32)
    gathered_rel = gather_relative(second_half, "prow", n_prow)
    own_pivot = lax.dynamic_slice_in_dim(lower_pivot, row_offset, own_rows, 0)
    upper_own = jnp.concatenate(
        [
            (
                pivot_masked[1, :, :half].astype(jnp.float32)
                - jnp.dot(own_pivot, gathered[0], preferred_element_type=jnp.float32)
            ).astype(jnp.bfloat16),
            (
                pivot_masked[1, :, half:].astype(jnp.float32)
                - jnp.dot(
                    jnp.roll(own_pivot, -row_offset, axis=1),
                    gathered_rel[0],
                    preferred_element_type=jnp.float32,
                )
            ).astype(jnp.bfloat16),
        ],
        1,
    )
    schur_second = masked[:, half:].astype(jnp.float32) - jnp.dot(
        multipliers_rel,
        gathered_rel.reshape(2 * block_size, col_count - half),
        preferred_element_type=jnp.float32,
    )
    schur_second = jnp.where(retained[None, half:], schur_second, jnp.zeros_like(schur_second))
    summed = jnp.concatenate([summed_first, grid_reduce_scatter(schur_second, "layer")], 1)
    ancestor = summed.reshape(1, 1, summed.shape[0], col_count)
    return (ancestor, lower_panel[None], upper_own[None])


def solution(mesh):
    placed = (
        P("layer", "prow", "pcol"),
        P("layer", None, "prow", "pcol"),
        P("layer", None, None, None),
        P("layer", "prow", "pcol"),
        P("layer", None, "pcol"),
    )
    return jax.shard_map(
        on_device,
        mesh=mesh,
        in_specs=placed,
        out_specs=(
            P("prow", "layer", None, "pcol"),
            P("layer", "prow", None),
            P("layer", "prow", "pcol"),
        ),
        check_vma=False,
    )
```

```python
import jax
import jax.numpy as jnp
from jax import lax
from jax.sharding import PartitionSpec as P


def ring(value, axis, size, step):
    return lax.ppermute(value, axis, [(i, (i + step) % size) for i in range(size)])


def gather_relative(value, axis, size):
    from_prev = ring(value, axis, size, 1)
    from_next = ring(value, axis, size, -1)
    half = value.shape[1] // 2
    far_lo = ring(from_prev[:, :half], axis, size, 1)
    far_hi = ring(from_next[:, half:], axis, size, -1)
    far = jnp.concatenate([far_lo, far_hi], 1)
    return jnp.concatenate([value, from_next, far, from_prev], 1)


def grid_shift(value, axis, side, dy, dx):
    pairs = []
    for y in range(side):
        for x in range(side):
            pairs.append((y * side + x, ((y + dy) % side) * side + (x + dx) % side))
    return lax.ppermute(value, axis, pairs)


def ring_reduce(blocks, send):
    half = blocks.shape[1] // 2
    far = blocks[2].astype(jnp.bfloat16)
    fwd1 = send(far[:half], 1)
    bwd1 = send(far[half:], -1)
    next_block = blocks[1]
    prev_block = blocks[3]
    fwd2 = send(
        jnp.concatenate([next_block[:half] + fwd1.astype(jnp.float32), next_block[half:]], 0).astype(
            jnp.bfloat16
        ),
        1,
    )
    bwd2 = send(
        jnp.concatenate([prev_block[:half], prev_block[half:] + bwd1.astype(jnp.float32)], 0).astype(
            jnp.bfloat16
        ),
        -1,
    )
    return blocks[0] + fwd2.astype(jnp.float32) + bwd2.astype(jnp.float32)


def relative(value, own, axis):
    return jnp.stack(
        [lax.dynamic_index_in_dim(value, (own + j) % 4, axis, keepdims=False) for j in range(4)], 0
    )


def grid_reduce_scatter(schur, axis):
    side = 4
    index = lax.axis_index(axis)
    gy = index // side
    gx = index % side
    rows, width = schur.shape
    part = rows // (side * side)
    grid = schur.reshape(side, side, part, width)
    left = grid[..., : width // 2]
    right = grid[..., width // 2 :]

    def along_x(v, step):
        return grid_shift(v, axis, side, 0, step)

    def along_y(v, step):
        return grid_shift(v, axis, side, step, 0)

    left = ring_reduce(relative(left, gx, 1), along_x)
    left = ring_reduce(relative(left, gy, 0), along_y)
    right = ring_reduce(relative(right, gy, 0), along_y)
    right = ring_reduce(relative(right, gx, 0), along_x)
    return jnp.concatenate([left, right], 1)


def on_device(front, pivots, inverses, slab_pattern, pivot_pattern):
    block_size = inverses.shape[-1]
    panel_width = 2 * block_size
    row_count = front.shape[1]
    col_count = front.shape[2]
    own_rows = pivots.shape[2]
    masked = (
        front[0].reshape(row_count // block_size, block_size, col_count // block_size, block_size)
        * slab_pattern[0].astype(jnp.bfloat16)[:, None, :, None]
    ).reshape(row_count, col_count)
    pivot_masked = (
        pivots[0].reshape(2, own_rows, col_count // block_size, block_size)
        * pivot_pattern[0].astype(jnp.bfloat16)[:, None, :, None]
    ).reshape(2, own_rows, col_count)
    first_inverse = inverses[0, 0]
    second_inverse = inverses[0, 1]
    row_offset = lax.axis_index("prow") * own_rows
    pcol = lax.axis_index("pcol")
    n_prow = lax.axis_size("prow")
    n_pcol = lax.axis_size("pcol")
    assert n_prow == 4
    half = (col_count * 11 // 16) // block_size * block_size
    gathered = lax.all_gather(pivot_masked[:, :, :half], "prow", axis=1, tiled=True)
    later_cols, gathered = lax.optimization_barrier((pivot_masked[:, :, half:], gathered))
    panel = jnp.roll(
        gather_relative(pivot_masked[:, :, :panel_width], "prow", n_prow), row_offset, axis=1
    )
    front_cols = masked[:, :panel_width]
    pivot_cols = panel[0]
    second_cols = panel[1]
    lower_pivot = jnp.dot(
        second_cols[:, :block_size], first_inverse, preferred_element_type=jnp.float32
    ).astype(jnp.bfloat16)
    lower_first = jnp.dot(
        front_cols[:, :block_size], first_inverse, preferred_element_type=jnp.float32
    ).astype(jnp.bfloat16)
    carried = (
        front_cols[:, block_size:].astype(jnp.float32)
        - jnp.dot(
            lower_first, pivot_cols[:, block_size:panel_width], preferred_element_type=jnp.float32
        )
    ).astype(jnp.bfloat16)
    lower_second = jnp.dot(carried, second_inverse, preferred_element_type=jnp.float32).astype(
        jnp.bfloat16
    )
    lower_panel = jnp.concatenate([lower_first, lower_second], 1)
    sent = lax.ppermute((lower_panel, lower_pivot), "pcol", [(0, i) for i in range(1, n_pcol)])
    on_root = pcol == 0
    lower_panel = jnp.where(on_root, lower_panel, sent[0])
    lower_pivot = jnp.where(on_root, lower_pivot, sent[1])
    folded = (
        lower_panel[:, :block_size].astype(jnp.float32)
        - jnp.dot(lower_panel[:, block_size:], lower_pivot, preferred_element_type=jnp.float32)
    ).astype(jnp.bfloat16)
    multipliers = jnp.concatenate([folded, lower_panel[:, block_size:]], 1)
    multipliers_rel = jnp.concatenate(
        [
            jnp.roll(folded, -row_offset, axis=1),
            jnp.roll(lower_panel[:, block_size:], -row_offset, axis=1),
        ],
        1,
    )
    col_index = pcol * col_count + jnp.arange(col_count, dtype=jnp.int32)
    retained = col_index >= panel_width
    schur_first = masked[:, :half].astype(jnp.float32) - jnp.dot(
        multipliers, gathered.reshape(2 * block_size, half), preferred_element_type=jnp.float32
    )
    schur_first = jnp.where(retained[None, :half], schur_first, jnp.zeros_like(schur_first))
    second_half = later_cols
    schur_first = schur_first.astype(jnp.bfloat16)
    summed_first = lax.psum_scatter(
        schur_first, "layer", scatter_dimension=0, tiled=True
    ).astype(jnp.float32)
    gathered_rel = gather_relative(second_half, "prow", n_prow)
    own_pivot = lax.dynamic_slice_in_dim(lower_pivot, row_offset, own_rows, 0)
    upper_own = jnp.concatenate(
        [
            (
                pivot_masked[1, :, :half].astype(jnp.float32)
                - jnp.dot(own_pivot, gathered[0], preferred_element_type=jnp.float32)
            ).astype(jnp.bfloat16),
            (
                pivot_masked[1, :, half:].astype(jnp.float32)
                - jnp.dot(
                    jnp.roll(own_pivot, -row_offset, axis=1),
                    gathered_rel[0],
                    preferred_element_type=jnp.float32,
                )
            ).astype(jnp.bfloat16),
        ],
        1,
    )
    schur_second = masked[:, half:].astype(jnp.float32) - jnp.dot(
        multipliers_rel,
        gathered_rel.reshape(2 * block_size, col_count - half),
        preferred_element_type=jnp.float32,
    )
    schur_second = jnp.where(retained[None, half:], schur_second, jnp.zeros_like(schur_second))
    summed = jnp.concatenate([summed_first, grid_reduce_scatter(schur_second, "layer")], 1)
    ancestor = summed.reshape(1, 1, summed.shape[0], col_count)
    return (ancestor, lower_panel[None], upper_own[None])


def solution(mesh):
    placed = (
        P("layer", "prow", "pcol"),
        P("layer", None, "prow", "pcol"),
        P("layer", None, None, None),
        P("layer", "prow", "pcol"),
        P("layer", None, "pcol"),
    )
    return jax.shard_map(
        on_device,
        mesh=mesh,
        in_specs=placed,
        out_specs=(
            P("prow", "layer", None, "pcol"),
            P("layer", "prow", None),
            P("layer", "prow", "pcol"),
        ),
        check_vma=False,
    )
```

```python
import jax
import jax.numpy as jnp
from jax import lax
from jax.sharding import PartitionSpec as P


def ring(value, axis, size, step):
    return lax.ppermute(value, axis, [(i, (i + step) % size) for i in range(size)])


def gather_relative(value, axis, size):
    from_prev = ring(value, axis, size, 1)
    from_next = ring(value, axis, size, -1)
    half = value.shape[1] // 2
    far_lo = ring(from_prev[:, :half], axis, size, 1)
    far_hi = ring(from_next[:, half:], axis, size, -1)
    far = jnp.concatenate([far_lo, far_hi], 1)
    return jnp.concatenate([value, from_next, far, from_prev], 1)


def grid_shift(value, axis, side, dy, dx):
    pairs = []
    for y in range(side):
        for x in range(side):
            pairs.append((y * side + x, ((y + dy) % side) * side + (x + dx) % side))
    return lax.ppermute(value, axis, pairs)


def ring_reduce(blocks, send):
    half = blocks.shape[1] // 2
    far = blocks[2].astype(jnp.bfloat16)
    fwd1 = send(far[:half], 1)
    bwd1 = send(far[half:], -1)
    next_block = blocks[1]
    prev_block = blocks[3]
    fwd2 = send(
        jnp.concatenate([next_block[:half] + fwd1.astype(jnp.float32), next_block[half:]], 0).astype(
            jnp.bfloat16
        ),
        1,
    )
    bwd2 = send(
        jnp.concatenate([prev_block[:half], prev_block[half:] + bwd1.astype(jnp.float32)], 0).astype(
            jnp.bfloat16
        ),
        -1,
    )
    return blocks[0] + fwd2.astype(jnp.float32) + bwd2.astype(jnp.float32)


def relative(value, own, axis):
    return jnp.stack(
        [lax.dynamic_index_in_dim(value, (own + j) % 4, axis, keepdims=False) for j in range(4)], 0
    )


def grid_reduce_scatter(left, right, axis):
    side = 4
    index = lax.axis_index(axis)
    gy = index // side
    gx = index % side
    rows, width = left.shape
    part = rows // (side * side)
    left = left.reshape(side, side, part, width)
    right = right.reshape(side, side, part, width)

    def along_x(v, step):
        return grid_shift(v, axis, side, 0, step)

    def along_y(v, step):
        return grid_shift(v, axis, side, step, 0)

    left = ring_reduce(relative(left, gx, 1), along_x)
    left = ring_reduce(relative(left, gy, 0), along_y)
    right = ring_reduce(relative(right, gy, 0), along_y)
    right = ring_reduce(relative(right, gx, 0), along_x)
    return jnp.concatenate([left, right], 1)


def on_device(front, pivots, inverses, slab_pattern, pivot_pattern):
    block_size = inverses.shape[-1]
    panel_width = 2 * block_size
    row_count = front.shape[1]
    col_count = front.shape[2]
    own_rows = pivots.shape[2]
    masked = (
        front[0].reshape(row_count // block_size, block_size, col_count // block_size, block_size)
        * slab_pattern[0].astype(jnp.bfloat16)[:, None, :, None]
    ).reshape(row_count, col_count)
    pivot_masked = (
        pivots[0].reshape(2, own_rows, col_count // block_size, block_size)
        * pivot_pattern[0].astype(jnp.bfloat16)[:, None, :, None]
    ).reshape(2, own_rows, col_count)
    first_inverse = inverses[0, 0]
    second_inverse = inverses[0, 1]
    row_offset = lax.axis_index("prow") * own_rows
    pcol = lax.axis_index("pcol")
    n_prow = lax.axis_size("prow")
    n_pcol = lax.axis_size("pcol")
    assert n_prow == 4
    half = (col_count * 11 // 16) // block_size * block_size
    gathered = lax.all_gather(pivot_masked[:, :, :half], "prow", axis=1, tiled=True)
    later_cols, gathered = lax.optimization_barrier((pivot_masked[:, :, half:], gathered))
    panel = jnp.roll(
        gather_relative(pivot_masked[:, :, :panel_width], "prow", n_prow), row_offset, axis=1
    )
    front_cols = masked[:, :panel_width]
    pivot_cols = panel[0]
    second_cols = panel[1]
    lower_pivot = jnp.dot(
        second_cols[:, :block_size], first_inverse, preferred_element_type=jnp.float32
    ).astype(jnp.bfloat16)
    lower_first = jnp.dot(
        front_cols[:, :block_size], first_inverse, preferred_element_type=jnp.float32
    ).astype(jnp.bfloat16)
    carried = (
        front_cols[:, block_size:].astype(jnp.float32)
        - jnp.dot(
            lower_first, pivot_cols[:, block_size:panel_width], preferred_element_type=jnp.float32
        )
    ).astype(jnp.bfloat16)
    lower_second = jnp.dot(carried, second_inverse, preferred_element_type=jnp.float32).astype(
        jnp.bfloat16
    )
    lower_panel = jnp.concatenate([lower_first, lower_second], 1)
    sent = lax.ppermute((lower_panel, lower_pivot), "pcol", [(0, i) for i in range(1, n_pcol)])
    on_root = pcol == 0
    lower_panel = jnp.where(on_root, lower_panel, sent[0])
    lower_pivot = jnp.where(on_root, lower_pivot, sent[1])
    folded = (
        lower_panel[:, :block_size].astype(jnp.float32)
        - jnp.dot(lower_panel[:, block_size:], lower_pivot, preferred_element_type=jnp.float32)
    ).astype(jnp.bfloat16)
    multipliers = jnp.concatenate([folded, lower_panel[:, block_size:]], 1)
    multipliers_rel = jnp.concatenate(
        [
            jnp.roll(folded, -row_offset, axis=1),
            jnp.roll(lower_panel[:, block_size:], -row_offset, axis=1),
        ],
        1,
    )
    col_index = pcol * col_count + jnp.arange(col_count, dtype=jnp.int32)
    retained = col_index >= panel_width
    schur_first = masked[:, :half].astype(jnp.float32) - jnp.dot(
        multipliers, gathered.reshape(2 * block_size, half), preferred_element_type=jnp.float32
    )
    schur_first = jnp.where(retained[None, :half], schur_first, jnp.zeros_like(schur_first))
    second_half = later_cols
    schur_first = schur_first.astype(jnp.bfloat16)
    summed_first = lax.psum_scatter(
        schur_first, "layer", scatter_dimension=0, tiled=True
    ).astype(jnp.float32)
    gathered_rel = gather_relative(second_half, "prow", n_prow)
    own_pivot = lax.dynamic_slice_in_dim(lower_pivot, row_offset, own_rows, 0)
    upper_own = jnp.concatenate(
        [
            (
                pivot_masked[1, :, :half].astype(jnp.float32)
                - jnp.dot(own_pivot, gathered[0], preferred_element_type=jnp.float32)
            ).astype(jnp.bfloat16),
            (
                pivot_masked[1, :, half:].astype(jnp.float32)
                - jnp.dot(
                    jnp.roll(own_pivot, -row_offset, axis=1),
                    gathered_rel[0],
                    preferred_element_type=jnp.float32,
                )
            ).astype(jnp.bfloat16),
        ],
        1,
    )
    split = (col_count - half) // 2
    stacked_rel = gathered_rel.reshape(2 * block_size, col_count - half)
    schur_halves = []
    for start in (0, split):
        cols = slice(half + start, half + start + split)
        schur_half = masked[:, cols].astype(jnp.float32) - jnp.dot(
            multipliers_rel, stacked_rel[:, start : start + split], preferred_element_type=jnp.float32
        )
        schur_halves.append(
            jnp.where(retained[None, cols], schur_half, jnp.zeros_like(schur_half))
        )
    summed = jnp.concatenate([summed_first, grid_reduce_scatter(*schur_halves, "layer")], 1)
    ancestor = summed.reshape(1, 1, summed.shape[0], col_count)
    return (ancestor, lower_panel[None], upper_own[None])


def solution(mesh):
    placed = (
        P("layer", "prow", "pcol"),
        P("layer", None, "prow", "pcol"),
        P("layer", None, None, None),
        P("layer", "prow", "pcol"),
        P("layer", None, "pcol"),
    )
    return jax.shard_map(
        on_device,
        mesh=mesh,
        in_specs=placed,
        out_specs=(
            P("prow", "layer", None, "pcol"),
            P("layer", "prow", None),
            P("layer", "prow", "pcol"),
        ),
        check_vma=False,
    )
```

```python
import jax
import jax.numpy as jnp
from jax import lax
from jax.sharding import PartitionSpec as P


def ring(value, axis, size, step):
    return lax.ppermute(value, axis, [(i, (i + step) % size) for i in range(size)])


def gather_relative(value, axis, size):
    from_prev = ring(value, axis, size, 1)
    from_next = ring(value, axis, size, -1)
    half = value.shape[1] // 2
    far_lo = ring(from_prev[:, :half], axis, size, 1)
    far_hi = ring(from_next[:, half:], axis, size, -1)
    far = jnp.concatenate([far_lo, far_hi], 1)
    return jnp.concatenate([value, from_next, far, from_prev], 1)


def grid_shift(value, axis, side, dy, dx):
    pairs = []
    for y in range(side):
        for x in range(side):
            pairs.append((y * side + x, ((y + dy) % side) * side + (x + dx) % side))
    return lax.ppermute(value, axis, pairs)


def ring_reduce(blocks, send):
    half = blocks.shape[1] // 2
    far = blocks[2].astype(jnp.bfloat16)
    fwd1 = send(far[:half], 1)
    bwd1 = send(far[half:], -1)
    next_block = blocks[1]
    prev_block = blocks[3]
    fwd2 = send(
        jnp.concatenate([next_block[:half] + fwd1.astype(jnp.float32), next_block[half:]], 0).astype(
            jnp.bfloat16
        ),
        1,
    )
    bwd2 = send(
        jnp.concatenate([prev_block[:half], prev_block[half:] + bwd1.astype(jnp.float32)], 0).astype(
            jnp.bfloat16
        ),
        -1,
    )
    return blocks[0] + fwd2.astype(jnp.float32) + bwd2.astype(jnp.float32)


def relative(value, own, axis):
    return jnp.stack(
        [lax.dynamic_index_in_dim(value, (own + j) % 4, axis, keepdims=False) for j in range(4)], 0
    )


def grid_reduce_scatter(left, right, axis):
    side = 4
    index = lax.axis_index(axis)
    gy = index // side
    gx = index % side
    rows, width = left.shape
    part = rows // (side * side)
    left = left.reshape(side, side, part, width)
    right = right.reshape(side, side, part, width)

    def along_x(v, step):
        return grid_shift(v, axis, side, 0, step)

    def along_y(v, step):
        return grid_shift(v, axis, side, step, 0)

    left = ring_reduce(relative(left, gx, 1), along_x)
    left = ring_reduce(relative(left, gy, 0), along_y)
    right = ring_reduce(relative(right, gy, 0), along_y)
    right = ring_reduce(relative(right, gx, 0), along_x)
    return jnp.concatenate([left, right], 1)


def on_device(front, pivots, inverses, slab_pattern, pivot_pattern):
    block_size = inverses.shape[-1]
    panel_width = 2 * block_size
    row_count = front.shape[1]
    col_count = front.shape[2]
    own_rows = pivots.shape[2]
    masked = (
        front[0].reshape(row_count // block_size, block_size, col_count // block_size, block_size)
        * slab_pattern[0].astype(jnp.bfloat16)[:, None, :, None]
    ).reshape(row_count, col_count)
    pivot_masked = (
        pivots[0].reshape(2, own_rows, col_count // block_size, block_size)
        * pivot_pattern[0].astype(jnp.bfloat16)[:, None, :, None]
    ).reshape(2, own_rows, col_count)
    first_inverse = inverses[0, 0]
    second_inverse = inverses[0, 1]
    row_offset = lax.axis_index("prow") * own_rows
    pcol = lax.axis_index("pcol")
    n_prow = lax.axis_size("prow")
    n_pcol = lax.axis_size("pcol")
    assert n_prow == 4
    half = (col_count * 11 // 16) // block_size * block_size
    gathered = lax.all_gather(pivots[0, :, :, :half], "prow", axis=1, tiled=True)
    gathered = (
        gathered.reshape(2, 4 * own_rows, half // block_size, block_size)
        * pivot_pattern[0, :, : half // block_size].astype(jnp.bfloat16)[:, None, :, None]
    ).reshape(2, 4 * own_rows, half)
    later_cols, gathered = lax.optimization_barrier((pivot_masked[:, :, half:], gathered))
    panel = jnp.roll(
        gather_relative(pivot_masked[:, :, :panel_width], "prow", n_prow), row_offset, axis=1
    )
    front_cols = masked[:, :panel_width]
    pivot_cols = panel[0]
    second_cols = panel[1]
    lower_pivot = jnp.dot(
        second_cols[:, :block_size], first_inverse, preferred_element_type=jnp.float32
    ).astype(jnp.bfloat16)
    lower_first = jnp.dot(
        front_cols[:, :block_size], first_inverse, preferred_element_type=jnp.float32
    ).astype(jnp.bfloat16)
    carried = (
        front_cols[:, block_size:].astype(jnp.float32)
        - jnp.dot(
            lower_first, pivot_cols[:, block_size:panel_width], preferred_element_type=jnp.float32
        )
    ).astype(jnp.bfloat16)
    lower_second = jnp.dot(carried, second_inverse, preferred_element_type=jnp.float32).astype(
        jnp.bfloat16
    )
    lower_panel = jnp.concatenate([lower_first, lower_second], 1)
    sent = lax.ppermute((lower_panel, lower_pivot), "pcol", [(0, i) for i in range(1, n_pcol)])
    on_root = pcol == 0
    lower_panel = jnp.where(on_root, lower_panel, sent[0])
    lower_pivot = jnp.where(on_root, lower_pivot, sent[1])
    folded = (
        lower_panel[:, :block_size].astype(jnp.float32)
        - jnp.dot(lower_panel[:, block_size:], lower_pivot, preferred_element_type=jnp.float32)
    ).astype(jnp.bfloat16)
    multipliers = jnp.concatenate([folded, lower_panel[:, block_size:]], 1)
    multipliers_rel = jnp.concatenate(
        [
            jnp.roll(folded, -row_offset, axis=1),
            jnp.roll(lower_panel[:, block_size:], -row_offset, axis=1),
        ],
        1,
    )
    col_index = pcol * col_count + jnp.arange(col_count, dtype=jnp.int32)
    retained = col_index >= panel_width
    schur_first = masked[:, :half].astype(jnp.float32) - jnp.dot(
        multipliers, gathered.reshape(2 * block_size, half), preferred_element_type=jnp.float32
    )
    schur_first = jnp.where(retained[None, :half], schur_first, jnp.zeros_like(schur_first))
    second_half = later_cols
    schur_first = schur_first.astype(jnp.bfloat16)
    summed_first = lax.psum_scatter(
        schur_first, "layer", scatter_dimension=0, tiled=True
    ).astype(jnp.float32)
    gathered_rel = gather_relative(second_half, "prow", n_prow)
    own_pivot = lax.dynamic_slice_in_dim(lower_pivot, row_offset, own_rows, 0)
    upper_own = jnp.concatenate(
        [
            (
                pivot_masked[1, :, :half].astype(jnp.float32)
                - jnp.dot(own_pivot, gathered[0], preferred_element_type=jnp.float32)
            ).astype(jnp.bfloat16),
            (
                pivot_masked[1, :, half:].astype(jnp.float32)
                - jnp.dot(
                    jnp.roll(own_pivot, -row_offset, axis=1),
                    gathered_rel[0],
                    preferred_element_type=jnp.float32,
                )
            ).astype(jnp.bfloat16),
        ],
        1,
    )
    split = (col_count - half) // 2
    stacked_rel = gathered_rel.reshape(2 * block_size, col_count - half)
    schur_halves = []
    for start in (0, split):
        cols = slice(half + start, half + start + split)
        schur_half = masked[:, cols].astype(jnp.float32) - jnp.dot(
            multipliers_rel, stacked_rel[:, start : start + split], preferred_element_type=jnp.float32
        )
        schur_halves.append(
            jnp.where(retained[None, cols], schur_half, jnp.zeros_like(schur_half))
        )
    summed = jnp.concatenate([summed_first, grid_reduce_scatter(*schur_halves, "layer")], 1)
    ancestor = summed.reshape(1, 1, summed.shape[0], col_count)
    return (ancestor, lower_panel[None], upper_own[None])


def solution(mesh):
    placed = (
        P("layer", "prow", "pcol"),
        P("layer", None, "prow", "pcol"),
        P("layer", None, None, None),
        P("layer", "prow", "pcol"),
        P("layer", None, "pcol"),
    )
    return jax.shard_map(
        on_device,
        mesh=mesh,
        in_specs=placed,
        out_specs=(
            P("prow", "layer", None, "pcol"),
            P("layer", "prow", None),
            P("layer", "prow", "pcol"),
        ),
        check_vma=False,
    )
```

```python
import jax
import jax.numpy as jnp
from jax import lax
from jax.sharding import PartitionSpec as P


def ring(value, axis, size, step):
    return lax.ppermute(value, axis, [(i, (i + step) % size) for i in range(size)])


def gather_relative(value, axis, size):
    from_prev = ring(value, axis, size, 1)
    from_next = ring(value, axis, size, -1)
    half = value.shape[1] // 2
    far_lo = ring(from_prev[:, :half], axis, size, 1)
    far_hi = ring(from_next[:, half:], axis, size, -1)
    far = jnp.concatenate([far_lo, far_hi], 1)
    return jnp.concatenate([value, from_next, far, from_prev], 1)


def grid_shift(value, axis, side, dy, dx):
    pairs = []
    for y in range(side):
        for x in range(side):
            pairs.append((y * side + x, ((y + dy) % side) * side + (x + dx) % side))
    return lax.ppermute(value, axis, pairs)


def ring_reduce(blocks, send):
    half = blocks.shape[1] // 2
    far = blocks[2].astype(jnp.bfloat16)
    fwd1 = send(far[:half], 1)
    bwd1 = send(far[half:], -1)
    next_block = blocks[1]
    prev_block = blocks[3]
    fwd2 = send(
        jnp.concatenate([next_block[:half] + fwd1.astype(jnp.float32), next_block[half:]], 0).astype(
            jnp.bfloat16
        ),
        1,
    )
    bwd2 = send(
        jnp.concatenate([prev_block[:half], prev_block[half:] + bwd1.astype(jnp.float32)], 0).astype(
            jnp.bfloat16
        ),
        -1,
    )
    return blocks[0] + fwd2.astype(jnp.float32) + bwd2.astype(jnp.float32)


def relative(value, own, axis):
    return jnp.stack(
        [lax.dynamic_index_in_dim(value, (own + j) % 4, axis, keepdims=False) for j in range(4)], 0
    )


def grid_reduce_scatter(left, right, axis):
    side = 4
    index = lax.axis_index(axis)
    gy = index // side
    gx = index % side
    rows, width = left.shape
    part = rows // (side * side)
    left = left.reshape(side, side, part, width)
    right = right.reshape(side, side, part, width)

    def along_x(v, step):
        return grid_shift(v, axis, side, 0, step)

    def along_y(v, step):
        return grid_shift(v, axis, side, step, 0)

    left = ring_reduce(relative(left, gx, 1), along_x)
    left = ring_reduce(relative(left, gy, 0), along_y)
    right = ring_reduce(relative(right, gy, 0), along_y)
    right = ring_reduce(relative(right, gx, 0), along_x)
    return jnp.concatenate([left, right], 1)


def on_device(front, pivots, inverses, slab_pattern, pivot_pattern):
    block_size = inverses.shape[-1]
    panel_width = 2 * block_size
    row_count = front.shape[1]
    col_count = front.shape[2]
    own_rows = pivots.shape[2]
    masked = (
        front[0].reshape(row_count // block_size, block_size, col_count // block_size, block_size)
        * slab_pattern[0].astype(jnp.bfloat16)[:, None, :, None]
    ).reshape(row_count, col_count)
    def mask_pivots(lo, hi):
        return (
            pivots[0, :, :, lo:hi].reshape(2, own_rows, (hi - lo) // block_size, block_size)
            * pivot_pattern[0, :, lo // block_size : hi // block_size].astype(jnp.bfloat16)[
                :, None, :, None
            ]
        ).reshape(2, own_rows, hi - lo)

    first_inverse = inverses[0, 0]
    second_inverse = inverses[0, 1]
    row_offset = lax.axis_index("prow") * own_rows
    pcol = lax.axis_index("pcol")
    n_prow = lax.axis_size("prow")
    n_pcol = lax.axis_size("pcol")
    assert n_prow == 4
    half = (col_count * 11 // 16) // block_size * block_size
    first_cols = mask_pivots(0, half)
    gathered = lax.all_gather(first_cols, "prow", axis=1, tiled=True)
    later_cols, gathered = lax.optimization_barrier((mask_pivots(half, col_count), gathered))
    panel = jnp.roll(
        gather_relative(first_cols[:, :, :panel_width], "prow", n_prow), row_offset, axis=1
    )
    front_cols = masked[:, :panel_width]
    pivot_cols = panel[0]
    second_cols = panel[1]
    lower_pivot = jnp.dot(
        second_cols[:, :block_size], first_inverse, preferred_element_type=jnp.float32
    ).astype(jnp.bfloat16)
    lower_first = jnp.dot(
        front_cols[:, :block_size], first_inverse, preferred_element_type=jnp.float32
    ).astype(jnp.bfloat16)
    carried = (
        front_cols[:, block_size:].astype(jnp.float32)
        - jnp.dot(
            lower_first, pivot_cols[:, block_size:panel_width], preferred_element_type=jnp.float32
        )
    ).astype(jnp.bfloat16)
    lower_second = jnp.dot(carried, second_inverse, preferred_element_type=jnp.float32).astype(
        jnp.bfloat16
    )
    lower_panel = jnp.concatenate([lower_first, lower_second], 1)
    sent = lax.ppermute((lower_panel, lower_pivot), "pcol", [(0, i) for i in range(1, n_pcol)])
    on_root = pcol == 0
    lower_panel = jnp.where(on_root, lower_panel, sent[0])
    lower_pivot = jnp.where(on_root, lower_pivot, sent[1])
    folded = (
        lower_panel[:, :block_size].astype(jnp.float32)
        - jnp.dot(lower_panel[:, block_size:], lower_pivot, preferred_element_type=jnp.float32)
    ).astype(jnp.bfloat16)
    multipliers = jnp.concatenate([folded, lower_panel[:, block_size:]], 1)
    multipliers_rel = jnp.concatenate(
        [
            jnp.roll(folded, -row_offset, axis=1),
            jnp.roll(lower_panel[:, block_size:], -row_offset, axis=1),
        ],
        1,
    )
    col_index = pcol * col_count + jnp.arange(col_count, dtype=jnp.int32)
    retained = col_index >= panel_width
    schur_first = masked[:, :half].astype(jnp.float32) - jnp.dot(
        multipliers, gathered.reshape(2 * block_size, half), preferred_element_type=jnp.float32
    )
    schur_first = jnp.where(retained[None, :half], schur_first, jnp.zeros_like(schur_first))
    second_half = later_cols
    schur_first = schur_first.astype(jnp.bfloat16)
    summed_first = lax.psum_scatter(
        schur_first, "layer", scatter_dimension=0, tiled=True
    ).astype(jnp.float32)
    gathered_rel = gather_relative(second_half, "prow", n_prow)
    own_pivot = lax.dynamic_slice_in_dim(lower_pivot, row_offset, own_rows, 0)
    upper_own = jnp.concatenate(
        [
            (
                first_cols[1].astype(jnp.float32)
                - jnp.dot(own_pivot, gathered[0], preferred_element_type=jnp.float32)
            ).astype(jnp.bfloat16),
            (
                later_cols[1].astype(jnp.float32)
                - jnp.dot(
                    jnp.roll(own_pivot, -row_offset, axis=1),
                    gathered_rel[0],
                    preferred_element_type=jnp.float32,
                )
            ).astype(jnp.bfloat16),
        ],
        1,
    )
    split = (col_count - half) // 2
    stacked_rel = gathered_rel.reshape(2 * block_size, col_count - half)
    schur_halves = []
    for start in (0, split):
        cols = slice(half + start, half + start + split)
        schur_half = masked[:, cols].astype(jnp.float32) - jnp.dot(
            multipliers_rel, stacked_rel[:, start : start + split], preferred_element_type=jnp.float32
        )
        schur_halves.append(
            jnp.where(retained[None, cols], schur_half, jnp.zeros_like(schur_half))
        )
    summed = jnp.concatenate([summed_first, grid_reduce_scatter(*schur_halves, "layer")], 1)
    ancestor = summed.reshape(1, 1, summed.shape[0], col_count)
    return (ancestor, lower_panel[None], upper_own[None])


def solution(mesh):
    placed = (
        P("layer", "prow", "pcol"),
        P("layer", None, "prow", "pcol"),
        P("layer", None, None, None),
        P("layer", "prow", "pcol"),
        P("layer", None, "pcol"),
    )
    return jax.shard_map(
        on_device,
        mesh=mesh,
        in_specs=placed,
        out_specs=(
            P("prow", "layer", None, "pcol"),
            P("layer", "prow", None),
            P("layer", "prow", "pcol"),
        ),
        check_vma=False,
    )
```
